128 devices in a mesh: ctx: 16 (over z_lo, y, core), ch: 8 (over z_hi, x).
Axes of the slice: x: 4, y: 4, z: 4 (z_hi: 2, z_lo: 2; z = z_hi * 2 + z_lo), core: 2. Of those that a mesh axis runs over, the one named last changes fastest.
Arguments:
- inputs: bfloat16 [512, 512, 1024], P('ctx', None, 'ch'), may hold values from -600 to 600
- norm_gain: float32 [1024], P('ch'), may hold values from 0.1 to 1.9
- conv_taps: float32 [2, 3, 1024], P(None, None, 'ch'), may hold values from -3 to 3
- factor_one: bfloat16 [512, 512], replicated, may hold values from -0.25 to 0.25
- factor_two: bfloat16 [512, 512], replicated, may hold values from -0.25 to 0.25
- kernel: bfloat16 [512, 512, 1024], P(None, 'ctx', 'ch'), may hold values from -5 to 5
- grad_out: bfloat16 [512, 512, 1024], P('ctx', None, 'ch'), may hold values from -5 to 5
Outputs:
- input_grad: bfloat16 [512, 512, 1024], P('ctx', None, 'ch')
- kernel_grad: bfloat16 [512, 512, 1024], P(None, 'ctx', 'ch')
- factor_one_grad: float32 [512, 512], replicated
- factor_two_grad: float32 [512, 512], replicated
- gain_grad: float32 [1024], P('ch')
- taps_grad: float32 [2, 3, 1024], P(None, None, 'ch')
The draws below stay inside these ranges and needn't reach their ends.
All inputs are finite; a program needn't handle non-finite values.
Results may differ from the reference program's by a relative error of at most 0.0081.
Values may be sent and summed in bfloat16 or wider, within the bound.
No kernel may reach another device: no remote copies, remote signals or barrier semaphores. Data moves between devices by JAX's collectives and lax.ppermute only.
A program may use at most 192 MiB of HBM per device.

```python
import math
import jax
import jax.numpy as jnp
from jax import lax

OUTER = 512
INNER = 512
WIDTH = 1024
TAPS = 3


def draw_inputs(key, part):
    key_base, key_rows, key_cols = jax.random.split(key, 3)
    base = jnp.clip(jax.random.normal(key_base, (OUTER, INNER, WIDTH), jnp.float32), -4.0, 4.0)
    row_scale = 10.0 ** jax.random.uniform(key_rows, (OUTER, INNER, 1), jnp.float32)
    col_scale = 10.0 ** (jnp.arange(WIDTH, dtype=jnp.float32) / WIDTH)
    col_scale = col_scale * jax.random.uniform(key_cols, (WIDTH,), jnp.float32, 0.7, 1.3)
    return (base * row_scale * col_scale).astype(jnp.bfloat16)


def block_scale(key, extent, cuts, least, high):
    level = 1.0
    for dim, parts in cuts:
        draws = jax.random.uniform(jax.random.fold_in(jax.random.fold_in(key, 6), dim), (parts,), jnp.float32, least / len(cuts), high / len(cuts))
        level = level * jnp.repeat(jnp.exp(draws), extent[dim] // parts).reshape((-1,) + (1,) * (len(extent) - 1 - dim))
    return level


def normal_values(key, shape, width, limit, pieces=(), held_as=jnp.bfloat16):
    level = block_scale(key, shape, pieces, -0.22, 0.18) if pieces else 1.0
    array = jax.random.normal(key, shape, jnp.float32) * width * level
    return jnp.minimum(jnp.maximum(array, -limit), limit).astype(held_as)


def setup_inputs(seed: int = 0) -> dict:
    keys = jax.random.split(jax.random.key(seed), 8)
    return {
        "inputs": draw_inputs(jax.random.fold_in(keys[7], 71), 0),
        "norm_gain": jnp.clip(1.0 + 0.18 * jax.random.normal(keys[1], (WIDTH,), jnp.float32), 0.1, 1.9),
        "conv_taps": normal_values(keys[2], (2, TAPS, WIDTH), 0.6, 3.0, ((2, 8),), jnp.float32),
        "factor_one": normal_values(keys[3], (INNER, INNER), INNER ** -0.5, 0.25),
        "factor_two": normal_values(keys[4], (OUTER, OUTER), OUTER ** -0.5, 0.25),
        "kernel": normal_values(keys[5], (OUTER, INNER, WIDTH), 1.0, 5.0, ((1, 16), (2, 8))),
        "grad_out": normal_values(keys[6], (OUTER, INNER, WIDTH), 1.0, 5.0, ((0, 16), (2, 8))),
    }


def reference(inputs, norm_gain, conv_taps, factor_one, factor_two, kernel, grad_out):
    length = OUTER * INNER
    group = math.gcd(WIDTH, 128)
    blocks = WIDTH // group
    wide = inputs.astype(jnp.float32)
    inverse = lax.rsqrt(lax.optimization_barrier(jnp.sum(wide * wide, axis=2)) / WIDTH + 1e-05)
    first = factor_one.astype(jnp.float32)
    second = factor_two.astype(jnp.float32)

    def block_work(start):
        piece_in = lax.dynamic_slice_in_dim(inputs, start, group, 2).astype(jnp.float32)
        hat = (piece_in * inverse[:, :, None]).reshape(length, group)
        gain = lax.dynamic_slice_in_dim(norm_gain, start, group, 0).astype(jnp.float32)
        taps = lax.dynamic_slice_in_dim(conv_taps, start, group, 2).astype(jnp.float32)
        kern = lax.dynamic_slice_in_dim(kernel, start, group, 2).astype(jnp.float32)
        cotan = lax.dynamic_slice_in_dim(grad_out, start, group, 2).astype(jnp.float32).reshape(length, group)
        normed = (hat * gain).astype(jnp.bfloat16)
        padded = jnp.concatenate([jnp.zeros((TAPS - 1, group), jnp.bfloat16), normed], 0).astype(jnp.float32)
        value_pre = jnp.zeros((length, group), jnp.float32)
        gate_pre = jnp.zeros((length, group), jnp.float32)
        for offset in range(TAPS):
            window = padded[TAPS - 1 - offset:TAPS - 1 - offset + length]
            value_pre = value_pre + taps[0, offset] * window
            gate_pre = gate_pre + taps[1, offset] * window
        mixed_in = value_pre.astype(jnp.bfloat16).reshape(OUTER, INNER, group).astype(jnp.float32)
        gate = jax.nn.sigmoid(gate_pre)
        section_one = jnp.einsum('ijc,jk->ikc', mixed_in, first).astype(jnp.bfloat16).astype(jnp.float32)
        spectrum = (section_one * kern).astype(jnp.bfloat16).astype(jnp.float32)
        section_two = jnp.einsum('ijc,ik->kjc', spectrum, second).astype(jnp.bfloat16).astype(jnp.float32)
        out_grad = (cotan * gate).astype(jnp.bfloat16).astype(jnp.float32).reshape(OUTER, INNER, group)
        grad_spec = jnp.einsum('kjc,ik->ijc', out_grad, second)
        kernel_part = (grad_spec * section_one).astype(jnp.bfloat16)
        grad_section = (grad_spec * kern).astype(jnp.bfloat16).astype(jnp.float32)
        two_part = jnp.einsum('ijc,kjc->ik', spectrum, out_grad)
        grad_gate_pre = cotan * section_two.reshape(length, group) * gate * (1.0 - gate)
        grad_mixed = jnp.einsum('ikc,jk->ijc', grad_section, first).reshape(length, group)
        one_part = jnp.einsum('ijc,ikc->jk', mixed_in, grad_section)
        zero_rows = jnp.zeros((TAPS - 1, group), jnp.float32)
        ext_value = jnp.concatenate([grad_mixed, zero_rows], 0)
        ext_gate = jnp.concatenate([grad_gate_pre, zero_rows], 0)
        grad_normed = jnp.zeros((length, group), jnp.float32)
        value_taps = []
        gate_taps = []
        for offset in range(TAPS):
            grad_normed = grad_normed + taps[0, offset] * ext_value[offset:offset + length]
            grad_normed = grad_normed + taps[1, offset] * ext_gate[offset:offset + length]
            window = padded[TAPS - 1 - offset:TAPS - 1 - offset + length]
            value_taps.append(lax.optimization_barrier(jnp.sum(grad_mixed * window, axis=0)))
            gate_taps.append(lax.optimization_barrier(jnp.sum(grad_gate_pre * window, axis=0)))
        tap_part = jnp.stack([jnp.stack(value_taps), jnp.stack(gate_taps)])
        gain_part = lax.optimization_barrier(jnp.sum(grad_normed * hat, axis=0))
        scaled = grad_normed * gain
        row_part = lax.optimization_barrier(jnp.sum(scaled * hat, axis=1))
        return (kernel_part, scaled, one_part, two_part, tap_part, gain_part, row_part)
    starts = jnp.arange(blocks, dtype=jnp.int32) * group
    kernel_parts, scaled_parts, one_parts, two_parts, tap_parts, gain_parts, row_parts = lax.map(block_work, starts)
    kernel_grad = jnp.moveaxis(kernel_parts, 0, 2).reshape(OUTER, INNER, WIDTH)
    scaled_all = jnp.moveaxis(scaled_parts, 0, 1).reshape(length, WIDTH)
    row_mean = lax.optimization_barrier(jnp.sum(row_parts, axis=0)) / WIDTH
    hat_all = (wide * inverse[:, :, None]).reshape(length, WIDTH)
    input_grad = (inverse.reshape(length, 1) * (scaled_all - hat_all * row_mean[:, None])).astype(jnp.bfloat16).reshape(OUTER, INNER, WIDTH)
    factor_one_grad = lax.optimization_barrier(jnp.sum(one_parts, axis=0)) / math.sqrt(OUTER * WIDTH)
    factor_two_grad = lax.optimization_barrier(jnp.sum(two_parts, axis=0)) / math.sqrt(INNER * WIDTH)
    gain_grad = gain_parts.reshape(WIDTH) / math.sqrt(length)
    taps_grad = jnp.moveaxis(tap_parts, 0, 2).reshape(2, TAPS, WIDTH) / math.sqrt(length)
    return (input_grad, kernel_grad, factor_one_grad, factor_two_grad, gain_grad, taps_grad)
```

```python
import math

import jax
import jax.numpy as jnp
from jax import lax
from jax.sharding import PartitionSpec as P

OUTER = 512
INNER = 512
WIDTH = 1024


def shifted(value, axis, steps):
    count = lax.axis_size(axis)
    initial, last = (max(0, -steps), min(count, count - steps))
    return lax.ppermute(value, axis, [(source, source + steps) for source in range(initial, last)])


def tree_psum(value, axis):
    count = lax.axis_size(axis)
    step = 1
    while step < count:
        pairs = [(source, source ^ step) for source in range(count)]
        value = jax.tree.map(lambda v, r: v + r, value, lax.ppermute(value, axis, pairs))
        step *= 2
    return value


def on_device(inputs, norm_gain, conv_taps, factor_one, factor_two, kernel, grad_out):
    local_outer, inner, chans = inputs.shape
    rows = local_outer * inner
    taps_count = conv_taps.shape[1]
    flat_in = inputs.reshape(rows, chans).astype(jnp.float32)
    squares = tree_psum(jnp.sum(flat_in * flat_in, axis=1), "ch")
    inverse = lax.rsqrt(squares / WIDTH + 1e-05)
    hat = flat_in * inverse[:, None]
    normed = (hat * norm_gain).astype(jnp.bfloat16)
    earlier = shifted(normed[rows - (taps_count - 1) :], "ctx", 1)
    extended = jnp.concatenate([earlier, normed], 0)
    value_pre = jnp.zeros((rows, chans), jnp.float32)
    gate_pre = jnp.zeros((rows, chans), jnp.float32)
    for offset in range(taps_count):
        window = extended[taps_count - 1 - offset : taps_count - 1 - offset + rows]
        value_pre = value_pre + conv_taps[0, offset] * window
        gate_pre = gate_pre + conv_taps[1, offset] * window
    mixed_in = value_pre.astype(jnp.bfloat16).reshape(local_outer, inner, chans)
    gate = jax.nn.sigmoid(gate_pre)
    cotangent = grad_out.reshape(rows, chans).astype(jnp.float32)
    section_one = jnp.einsum(
        "ijc,jk->ikc", mixed_in, factor_one, preferred_element_type=jnp.float32
    ).astype(jnp.bfloat16)
    out_grad = (cotangent * gate).astype(jnp.bfloat16).reshape(local_outer, inner, chans)
    columns = lax.all_to_all(section_one, "ctx", split_axis=1, concat_axis=0, tiled=True)
    kern = kernel.astype(jnp.float32)
    spectrum = (columns.astype(jnp.float32) * kern).astype(jnp.bfloat16)
    section_two = jnp.einsum(
        "ijc,ik->kjc", spectrum, factor_two, preferred_element_type=jnp.float32
    ).astype(jnp.bfloat16)
    back_rows = lax.all_to_all(section_two, "ctx", split_axis=0, concat_axis=1, tiled=True)
    grad_columns = lax.all_to_all(out_grad, "ctx", split_axis=1, concat_axis=0, tiled=True)
    grad_spec = jnp.einsum(
        "kjc,ik->ijc", grad_columns, factor_two, preferred_element_type=jnp.float32
    )
    kernel_grad = (grad_spec * columns.astype(jnp.float32)).astype(jnp.bfloat16)
    grad_section = (grad_spec * kern).astype(jnp.bfloat16)
    two_part = jnp.einsum("ijc,kjc->ik", spectrum, grad_columns, preferred_element_type=jnp.float32)
    two_total = lax.psum(two_part, ("ctx", "ch"))
    grad_rows = lax.all_to_all(grad_section, "ctx", split_axis=0, concat_axis=1, tiled=True)
    back_flat = back_rows.reshape(rows, chans).astype(jnp.float32)
    grad_gate_pre = cotangent * back_flat * gate * (1.0 - gate)
    grad_mixed = jnp.einsum(
        "ikc,jk->ijc", grad_rows, factor_one, preferred_element_type=jnp.float32
    ).reshape(rows, chans)
    one_part = jnp.einsum("ijc,ikc->jk", mixed_in, grad_rows, preferred_element_type=jnp.float32)
    two_total, one_part = lax.optimization_barrier((two_total, one_part))
    one_total = lax.psum(one_part, ("ctx", "ch"))
    later_value, later_gate = shifted(
        (grad_mixed[: taps_count - 1], grad_gate_pre[: taps_count - 1]), "ctx", -1
    )
    ext_value = jnp.concatenate([grad_mixed, later_value], 0)
    ext_gate = jnp.concatenate([grad_gate_pre, later_gate], 0)
    grad_normed = jnp.zeros((rows, chans), jnp.float32)
    value_taps = []
    gate_taps = []
    for offset in range(taps_count):
        grad_normed = grad_normed + conv_taps[0, offset] * ext_value[offset : offset + rows]
        grad_normed = grad_normed + conv_taps[1, offset] * ext_gate[offset : offset + rows]
        window = extended[taps_count - 1 - offset : taps_count - 1 - offset + rows]
        value_taps.append(jnp.sum(grad_mixed * window, axis=0))
        gate_taps.append(jnp.sum(grad_gate_pre * window, axis=0))
    tap_part = jnp.stack([jnp.stack(value_taps), jnp.stack(gate_taps)])
    gain_part = jnp.sum(grad_normed * hat, axis=0)
    gain_total, taps_total = tree_psum((gain_part, tap_part), "ctx")
    scaled = grad_normed * norm_gain
    row_mean = (
        tree_psum(jnp.sum(scaled * hat, axis=1), "ch")
        / WIDTH
    )
    input_grad = (
        (inverse[:, None] * (scaled - hat * row_mean[:, None]))
        .astype(jnp.bfloat16)
        .reshape(local_outer, inner, chans)
    )
    seq_scale = 1.0 / math.sqrt(OUTER * INNER)
    factor_one_grad = one_total / math.sqrt(OUTER * WIDTH)
    factor_two_grad = two_total / math.sqrt(INNER * WIDTH)
    return (
        input_grad,
        kernel_grad,
        factor_one_grad,
        factor_two_grad,
        gain_total * seq_scale,
        taps_total * seq_scale,
    )


def solution(mesh):
    in_specs = (
        P("ctx", None, "ch"),
        P("ch"),
        P(None, None, "ch"),
        P(),
        P(),
        P(None, "ctx", "ch"),
        P("ctx", None, "ch"),
    )
    out_specs = (P("ctx", None, "ch"), P(None, "ctx", "ch"), P(), P(), P("ch"), P(None, None, "ch"))
    return jax.shard_map(
        on_device, mesh=mesh, in_specs=in_specs, out_specs=out_specs, check_vma=False
    )
```

```python
import math

import jax
import jax.numpy as jnp
from jax import lax
from jax.sharding import PartitionSpec as P

OUTER = 512
INNER = 512
WIDTH = 1024


def shifted(value, axis, steps):
    count = lax.axis_size(axis)
    initial, last = (max(0, -steps), min(count, count - steps))
    return lax.ppermute(value, axis, [(source, source + steps) for source in range(initial, last)])


def tree_psum(value, axis):
    count = lax.axis_size(axis)
    step = 1
    while step < count:
        pairs = [(source, source ^ step) for source in range(count)]
        value = jax.tree.map(lambda v, r: v + r, value, lax.ppermute(value, axis, pairs))
        step *= 2
    return value


def exchange(value, axis, step):
    count = lax.axis_size(axis)
    return lax.ppermute(value, axis, [(source, source ^ step) for source in range(count)])


def tree_allreduce(value, rounds):
    kept = []
    for axis, step in rounds:
        upper = (lax.axis_index(axis) // step) % 2 == 1
        half = value.shape[0] // 2
        low, high = value[:half], value[half:]
        keep = jnp.where(upper, high, low)
        value = keep + exchange(jnp.where(upper, low, high), axis, step)
        kept.append((axis, step, upper))
    for axis, step, upper in reversed(kept):
        other = exchange(value, axis, step)
        value = jnp.where(
            upper, jnp.concatenate([other, value]), jnp.concatenate([value, other])
        )
    return value


FACTOR_ROUNDS = (("ctx", 1), ("ctx", 2), ("ch", 1), ("ctx", 8), ("ctx", 4), ("ch", 2), ("ch", 4))


def on_device(inputs, norm_gain, conv_taps, factor_one, factor_two, kernel, grad_out):
    local_outer, inner, chans = inputs.shape
    rows = local_outer * inner
    taps_count = conv_taps.shape[1]
    flat_in = inputs.reshape(rows, chans).astype(jnp.float32)
    squares = tree_psum(jnp.sum(flat_in * flat_in, axis=1), "ch")
    inverse = lax.rsqrt(squares / WIDTH + 1e-05)
    hat = flat_in * inverse[:, None]
    normed = (hat * norm_gain).astype(jnp.bfloat16)
    earlier = shifted(normed[rows - (taps_count - 1) :], "ctx", 1)
    extended = jnp.concatenate([earlier, normed], 0)
    value_pre = jnp.zeros((rows, chans), jnp.float32)
    gate_pre = jnp.zeros((rows, chans), jnp.float32)
    for offset in range(taps_count):
        window = extended[taps_count - 1 - offset : taps_count - 1 - offset + rows]
        value_pre = value_pre + conv_taps[0, offset] * window
        gate_pre = gate_pre + conv_taps[1, offset] * window
    mixed_in = value_pre.astype(jnp.bfloat16).reshape(local_outer, inner, chans)
    gate = jax.nn.sigmoid(gate_pre)
    cotangent = grad_out.reshape(rows, chans).astype(jnp.float32)
    section_one = jnp.einsum(
        "ijc,jk->ikc", mixed_in, factor_one, preferred_element_type=jnp.float32
    ).astype(jnp.bfloat16)
    out_grad = (cotangent * gate).astype(jnp.bfloat16).reshape(local_outer, inner, chans)
    columns = lax.all_to_all(section_one, "ctx", split_axis=1, concat_axis=0, tiled=True)
    kern = kernel.astype(jnp.float32)
    spectrum = (columns.astype(jnp.float32) * kern).astype(jnp.bfloat16)
    section_two = jnp.einsum(
        "ijc,ik->kjc", spectrum, factor_two, preferred_element_type=jnp.float32
    ).astype(jnp.bfloat16)
    back_rows = lax.all_to_all(section_two, "ctx", split_axis=0, concat_axis=1, tiled=True)
    grad_columns = lax.all_to_all(out_grad, "ctx", split_axis=1, concat_axis=0, tiled=True)
    grad_spec = jnp.einsum(
        "kjc,ik->ijc", grad_columns, factor_two, preferred_element_type=jnp.float32
    )
    kernel_grad = (grad_spec * columns.astype(jnp.float32)).astype(jnp.bfloat16)
    grad_section = (grad_spec * kern).astype(jnp.bfloat16)
    two_part = jnp.einsum("ijc,kjc->ik", spectrum, grad_columns, preferred_element_type=jnp.float32)
    two_total = tree_allreduce(two_part, FACTOR_ROUNDS)
    grad_rows = lax.all_to_all(grad_section, "ctx", split_axis=0, concat_axis=1, tiled=True)
    back_flat = back_rows.reshape(rows, chans).astype(jnp.float32)
    grad_gate_pre = cotangent * back_flat * gate * (1.0 - gate)
    grad_mixed = jnp.einsum(
        "ikc,jk->ijc", grad_rows, factor_one, preferred_element_type=jnp.float32
    ).reshape(rows, chans)
    one_part = jnp.einsum("ijc,ikc->jk", mixed_in, grad_rows, preferred_element_type=jnp.float32)
    one_total = tree_allreduce(one_part, FACTOR_ROUNDS)
    later_value, later_gate = shifted(
        (grad_mixed[: taps_count - 1], grad_gate_pre[: taps_count - 1]), "ctx", -1
    )
    ext_value = jnp.concatenate([grad_mixed, later_value], 0)
    ext_gate = jnp.concatenate([grad_gate_pre, later_gate], 0)
    grad_normed = jnp.zeros((rows, chans), jnp.float32)
    value_taps = []
    gate_taps = []
    for offset in range(taps_count):
        grad_normed = grad_normed + conv_taps[0, offset] * ext_value[offset : offset + rows]
        grad_normed = grad_normed + conv_taps[1, offset] * ext_gate[offset : offset + rows]
        window = extended[taps_count - 1 - offset : taps_count - 1 - offset + rows]
        value_taps.append(jnp.sum(grad_mixed * window, axis=0))
        gate_taps.append(jnp.sum(grad_gate_pre * window, axis=0))
    tap_part = jnp.stack([jnp.stack(value_taps), jnp.stack(gate_taps)])
    gain_part = jnp.sum(grad_normed * hat, axis=0)
    gain_total, taps_total = tree_psum((gain_part, tap_part), "ctx")
    scaled = grad_normed * norm_gain
    row_mean = (
        tree_psum(jnp.sum(scaled * hat, axis=1), "ch")
        / WIDTH
    )
    input_grad = (
        (inverse[:, None] * (scaled - hat * row_mean[:, None]))
        .astype(jnp.bfloat16)
        .reshape(local_outer, inner, chans)
    )
    seq_scale = 1.0 / math.sqrt(OUTER * INNER)
    factor_one_grad = one_total / math.sqrt(OUTER * WIDTH)
    factor_two_grad = two_total / math.sqrt(INNER * WIDTH)
    return (
        input_grad,
        kernel_grad,
        factor_one_grad,
        factor_two_grad,
        gain_total * seq_scale,
        taps_total * seq_scale,
    )


def solution(mesh):
    in_specs = (
        P("ctx", None, "ch"),
        P("ch"),
        P(None, None, "ch"),
        P(),
        P(),
        P(None, "ctx", "ch"),
        P("ctx", None, "ch"),
    )
    out_specs = (P("ctx", None, "ch"), P(None, "ctx", "ch"), P(), P(), P("ch"), P(None, None, "ch"))
    return jax.shard_map(
        on_device, mesh=mesh, in_specs=in_specs, out_specs=out_specs, check_vma=False
    )
```

```python
import math

import jax
import jax.numpy as jnp
from jax import lax
from jax.sharding import PartitionSpec as P

OUTER = 512
INNER = 512
WIDTH = 1024


def shifted(value, axis, steps):
    count = lax.axis_size(axis)
    initial, last = (max(0, -steps), min(count, count - steps))
    return lax.ppermute(value, axis, [(source, source + steps) for source in range(initial, last)])


def tree_psum(value, axis):
    count = lax.axis_size(axis)
    step = 1
    while step < count:
        pairs = [(source, source ^ step) for source in range(count)]
        value = jax.tree.map(lambda v, r: v + r, value, lax.ppermute(value, axis, pairs))
        step *= 2
    return value


def exchange(value, axis, step):
    count = lax.axis_size(axis)
    return lax.ppermute(value, axis, [(source, source ^ step) for source in range(count)])


def tree_allreduce(value, rounds):
    kept = []
    for axis, step in rounds:
        upper = (lax.axis_index(axis) // step) % 2 == 1
        half = value.shape[0] // 2
        low, high = value[:half], value[half:]
        keep = jnp.where(upper, high, low)
        value = keep + exchange(jnp.where(upper, low, high), axis, step)
        kept.append((axis, step, upper))
    for axis, step, upper in reversed(kept):
        other = exchange(value, axis, step)
        value = jnp.where(
            upper, jnp.concatenate([other, value]), jnp.concatenate([value, other])
        )
    return value


FACTOR_ROUNDS = (("ctx", 1), ("ctx", 2), ("ch", 1), ("ctx", 8), ("ctx", 4), ("ch", 2), ("ch", 4))


def on_device(inputs, norm_gain, conv_taps, factor_one, factor_two, kernel, grad_out):
    local_outer, inner, chans = inputs.shape
    rows = local_outer * inner
    taps_count = conv_taps.shape[1]
    flat_in = inputs.reshape(rows, chans).astype(jnp.float32)
    squares = tree_psum(jnp.sum(flat_in * flat_in, axis=1), "ch")
    inverse = lax.rsqrt(squares / WIDTH + 1e-05)
    hat = flat_in * inverse[:, None]
    normed = (hat * norm_gain).astype(jnp.bfloat16)
    earlier = shifted(normed[rows - (taps_count - 1) :], "ctx", 1)
    extended = jnp.concatenate([earlier, normed], 0)
    value_pre = jnp.zeros((rows, chans), jnp.float32)
    gate_pre = jnp.zeros((rows, chans), jnp.float32)
    for offset in range(taps_count):
        window = extended[taps_count - 1 - offset : taps_count - 1 - offset + rows]
        value_pre = value_pre + conv_taps[0, offset] * window
        gate_pre = gate_pre + conv_taps[1, offset] * window
    mixed_in = value_pre.astype(jnp.bfloat16).reshape(local_outer, inner, chans)
    gate = jax.nn.sigmoid(gate_pre)
    cotangent = grad_out.reshape(rows, chans).astype(jnp.float32)
    section_one = jnp.einsum(
        "ijc,jk->ikc", mixed_in, factor_one, preferred_element_type=jnp.float32
    ).astype(jnp.bfloat16)
    out_grad = (cotangent * gate).astype(jnp.bfloat16).reshape(local_outer, inner, chans)
    columns = lax.all_to_all(section_one, "ctx", split_axis=1, concat_axis=0, tiled=True)
    kern = kernel.astype(jnp.float32)
    spectrum = (columns.astype(jnp.float32) * kern).astype(jnp.bfloat16)
    section_two = jnp.einsum(
        "ijc,ik->kjc", spectrum, factor_two, preferred_element_type=jnp.float32
    ).astype(jnp.bfloat16)
    back_rows = lax.all_to_all(section_two, "ctx", split_axis=0, concat_axis=1, tiled=True)
    grad_columns = lax.all_to_all(out_grad, "ctx", split_axis=1, concat_axis=0, tiled=True)
    grad_spec = jnp.einsum(
        "kjc,ik->ijc", grad_columns, factor_two, preferred_element_type=jnp.float32
    )
    kernel_grad = (grad_spec * columns.astype(jnp.float32)).astype(jnp.bfloat16)
    grad_section = (grad_spec * kern).astype(jnp.bfloat16)
    two_part = jnp.einsum("ijc,kjc->ik", spectrum, grad_columns, preferred_element_type=jnp.float32)
    two_total = tree_allreduce(two_part, FACTOR_ROUNDS)
    back_rows, grad_section = lax.optimization_barrier((back_rows, grad_section))
    grad_rows = lax.all_to_all(grad_section, "ctx", split_axis=0, concat_axis=1, tiled=True)
    back_flat = back_rows.reshape(rows, chans).astype(jnp.float32)
    grad_gate_pre = cotangent * back_flat * gate * (1.0 - gate)
    grad_mixed = jnp.einsum(
        "ikc,jk->ijc", grad_rows, factor_one, preferred_element_type=jnp.float32
    ).reshape(rows, chans)
    one_part = jnp.einsum("ijc,ikc->jk", mixed_in, grad_rows, preferred_element_type=jnp.float32)
    one_total = tree_allreduce(one_part, FACTOR_ROUNDS)
    later_value, later_gate = shifted(
        (grad_mixed[: taps_count - 1], grad_gate_pre[: taps_count - 1]), "ctx", -1
    )
    ext_value = jnp.concatenate([grad_mixed, later_value], 0)
    ext_gate = jnp.concatenate([grad_gate_pre, later_gate], 0)
    grad_normed = jnp.zeros((rows, chans), jnp.float32)
    value_taps = []
    gate_taps = []
    for offset in range(taps_count):
        grad_normed = grad_normed + conv_taps[0, offset] * ext_value[offset : offset + rows]
        grad_normed = grad_normed + conv_taps[1, offset] * ext_gate[offset : offset + rows]
        window = extended[taps_count - 1 - offset : taps_count - 1 - offset + rows]
        value_taps.append(jnp.sum(grad_mixed * window, axis=0))
        gate_taps.append(jnp.sum(grad_gate_pre * window, axis=0))
    tap_part = jnp.stack([jnp.stack(value_taps), jnp.stack(gate_taps)])
    gain_part = jnp.sum(grad_normed * hat, axis=0)
    gain_total, taps_total = tree_psum((gain_part, tap_part), "ctx")
    scaled = grad_normed * norm_gain
    row_mean = (
        tree_psum(jnp.sum(scaled * hat, axis=1), "ch")
        / WIDTH
    )
    input_grad = (
        (inverse[:, None] * (scaled - hat * row_mean[:, None]))
        .astype(jnp.bfloat16)
        .reshape(local_outer, inner, chans)
    )
    seq_scale = 1.0 / math.sqrt(OUTER * INNER)
    factor_one_grad = one_total / math.sqrt(OUTER * WIDTH)
    factor_two_grad = two_total / math.sqrt(INNER * WIDTH)
    return (
        input_grad,
        kernel_grad,
        factor_one_grad,
        factor_two_grad,
        gain_total * seq_scale,
        taps_total * seq_scale,
    )


def solution(mesh):
    in_specs = (
        P("ctx", None, "ch"),
        P("ch"),
        P(None, None, "ch"),
        P(),
        P(),
        P(None, "ctx", "ch"),
        P("ctx", None, "ch"),
    )
    out_specs = (P("ctx", None, "ch"), P(None, "ctx", "ch"), P(), P(), P("ch"), P(None, None, "ch"))
    return jax.shard_map(
        on_device, mesh=mesh, in_specs=in_specs, out_specs=out_specs, check_vma=False
    )
```

```python
import math

import jax
import jax.numpy as jnp
from jax import lax
from jax.sharding import PartitionSpec as P

OUTER = 512
INNER = 512
WIDTH = 1024


def shifted(value, axis, steps):
    count = lax.axis_size(axis)
    initial, last = (max(0, -steps), min(count, count - steps))
    return lax.ppermute(value, axis, [(source, source + steps) for source in range(initial, last)])


def tree_psum(value, axis):
    count = lax.axis_size(axis)
    step = 1
    while step < count:
        pairs = [(source, source ^ step) for source in range(count)]
        value = jax.tree.map(lambda v, r: v + r, value, lax.ppermute(value, axis, pairs))
        step *= 2
    return value


def exchange(value, axis, step):
    count = lax.axis_size(axis)
    return lax.ppermute(value, axis, [(source, source ^ step) for source in range(count)])


def tree_allreduce(value, rounds):
    kept = []
    for axis, step in rounds:
        upper = (lax.axis_index(axis) // step) % 2 == 1
        half = value.shape[0] // 2
        low, high = value[:half], value[half:]
        keep = jnp.where(upper, high, low)
        value = keep + exchange(jnp.where(upper, low, high), axis, step)
        kept.append((axis, step, upper))
    for axis, step, upper in reversed(kept):
        other = exchange(value, axis, step)
        value = jnp.where(
            upper, jnp.concatenate([other, value]), jnp.concatenate([value, other])
        )
    return value


FACTOR_ROUNDS = (("ctx", 1), ("ctx", 2), ("ch", 1), ("ctx", 8), ("ctx", 4), ("ch", 2), ("ch", 4))


def on_device(inputs, norm_gain, conv_taps, factor_one, factor_two, kernel, grad_out):
    local_outer, inner, chans = inputs.shape
    rows = local_outer * inner
    taps_count = conv_taps.shape[1]
    flat_in = inputs.reshape(rows, chans).astype(jnp.float32)
    squares = tree_psum(jnp.sum(flat_in * flat_in, axis=1), "ch")
    inverse = lax.rsqrt(squares / WIDTH + 1e-05)
    hat = flat_in * inverse[:, None]
    normed = (hat * norm_gain).astype(jnp.bfloat16)
    earlier = shifted(normed[rows - (taps_count - 1) :], "ctx", 1)
    extended = jnp.concatenate([earlier, normed], 0)
    value_pre = jnp.zeros((rows, chans), jnp.float32)
    gate_pre = jnp.zeros((rows, chans), jnp.float32)
    for offset in range(taps_count):
        window = extended[taps_count - 1 - offset : taps_count - 1 - offset + rows]
        value_pre = value_pre + conv_taps[0, offset] * window
        gate_pre = gate_pre + conv_taps[1, offset] * window
    mixed_in = value_pre.astype(jnp.bfloat16).reshape(local_outer, inner, chans)
    gate = jax.nn.sigmoid(gate_pre)
    cotangent = grad_out.reshape(rows, chans).astype(jnp.float32)
    section_one = jnp.einsum(
        "ijc,jk->ikc", mixed_in, factor_one, preferred_element_type=jnp.float32
    ).astype(jnp.bfloat16)
    out_grad = (cotangent * gate).astype(jnp.bfloat16).reshape(local_outer, inner, chans)
    columns = lax.all_to_all(section_one, "ctx", split_axis=1, concat_axis=0, tiled=True)
    kern = kernel.astype(jnp.float32)
    spectrum = (columns.astype(jnp.float32) * kern).astype(jnp.bfloat16)
    section_two = jnp.einsum(
        "ijc,ik->kjc", spectrum, factor_two, preferred_element_type=jnp.float32
    ).astype(jnp.bfloat16)
    back_rows = lax.all_to_all(section_two, "ctx", split_axis=0, concat_axis=1, tiled=True)
    grad_columns = lax.all_to_all(out_grad, "ctx", split_axis=1, concat_axis=0, tiled=True)
    grad_spec = jnp.einsum(
        "kjc,ik->ijc", grad_columns, factor_two, preferred_element_type=jnp.float32
    )
    kernel_grad = (grad_spec * columns.astype(jnp.float32)).astype(jnp.bfloat16)
    grad_section = (grad_spec * kern).astype(jnp.bfloat16)
    two_part = jnp.einsum("ijc,kjc->ik", spectrum, grad_columns, preferred_element_type=jnp.float32)
    two_total = tree_allreduce(two_part, FACTOR_ROUNDS)
    back_rows, grad_section = lax.optimization_barrier((back_rows, grad_section))
    grad_rows = lax.all_to_all(grad_section, "ctx", split_axis=0, concat_axis=1, tiled=True)
    back_flat = back_rows.reshape(rows, chans).astype(jnp.float32)
    grad_gate_pre = cotangent * back_flat * gate * (1.0 - gate)
    later_gate = shifted(grad_gate_pre[: taps_count - 1], "ctx", -1)
    ext_gate = jnp.concatenate([grad_gate_pre, later_gate], 0)
    gate_normed = jnp.zeros((rows, chans), jnp.float32)
    gate_taps = []
    for offset in range(taps_count):
        gate_normed = gate_normed + conv_taps[1, offset] * ext_gate[offset : offset + rows]
        window = extended[taps_count - 1 - offset : taps_count - 1 - offset + rows]
        gate_taps.append(jnp.sum(grad_gate_pre * window, axis=0))
    gate_normed, gate_taps, grad_rows = lax.optimization_barrier((gate_normed, gate_taps, grad_rows))
    grad_mixed = jnp.einsum(
        "ikc,jk->ijc", grad_rows, factor_one, preferred_element_type=jnp.float32
    ).reshape(rows, chans)
    one_part = jnp.einsum("ijc,ikc->jk", mixed_in, grad_rows, preferred_element_type=jnp.float32)
    one_total = tree_allreduce(one_part, FACTOR_ROUNDS)
    grad_mixed = lax.optimization_barrier(grad_mixed)
    later_value = shifted(grad_mixed[: taps_count - 1], "ctx", -1)
    ext_value = jnp.concatenate([grad_mixed, later_value], 0)
    grad_normed = gate_normed
    value_taps = []
    for offset in range(taps_count):
        grad_normed = grad_normed + conv_taps[0, offset] * ext_value[offset : offset + rows]
        window = extended[taps_count - 1 - offset : taps_count - 1 - offset + rows]
        value_taps.append(jnp.sum(grad_mixed * window, axis=0))
    tap_part = jnp.stack([jnp.stack(value_taps), jnp.stack(gate_taps)])
    gain_part = jnp.sum(grad_normed * hat, axis=0)
    gain_total, taps_total = tree_psum((gain_part, tap_part), "ctx")
    scaled = grad_normed * norm_gain
    row_mean = (
        tree_psum(jnp.sum(scaled * hat, axis=1), "ch")
        / WIDTH
    )
    input_grad = (
        (inverse[:, None] * (scaled - hat * row_mean[:, None]))
        .astype(jnp.bfloat16)
        .reshape(local_outer, inner, chans)
    )
    seq_scale = 1.0 / math.sqrt(OUTER * INNER)
    factor_one_grad = one_total / math.sqrt(OUTER * WIDTH)
    factor_two_grad = two_total / math.sqrt(INNER * WIDTH)
    return (
        input_grad,
        kernel_grad,
        factor_one_grad,
        factor_two_grad,
        gain_total * seq_scale,
        taps_total * seq_scale,
    )


def solution(mesh):
    in_specs = (
        P("ctx", None, "ch"),
        P("ch"),
        P(None, None, "ch"),
        P(),
        P(),
        P(None, "ctx", "ch"),
        P("ctx", None, "ch"),
    )
    out_specs = (P("ctx", None, "ch"), P(None, "ctx", "ch"), P(), P(), P("ch"), P(None, None, "ch"))
    return jax.shard_map(
        on_device, mesh=mesh, in_specs=in_specs, out_specs=out_specs, check_vma=False
    )
```

```python
import math

import jax
import jax.numpy as jnp
from jax import lax
from jax.sharding import PartitionSpec as P

OUTER = 512
INNER = 512
WIDTH = 1024


def shifted(value, axis, steps):
    count = lax.axis_size(axis)
    initial, last = (max(0, -steps), min(count, count - steps))
    return lax.ppermute(value, axis, [(source, source + steps) for source in range(initial, last)])


def tree_psum(value, axis):
    count = lax.axis_size(axis)
    step = 1
    while step < count:
        pairs = [(source, source ^ step) for source in range(count)]
        value = jax.tree.map(lambda v, r: v + r, value, lax.ppermute(value, axis, pairs))
        step *= 2
    return value


def exchange(value, axis, step):
    count = lax.axis_size(axis)
    return lax.ppermute(value, axis, [(source, source ^ step) for source in range(count)])


def tree_allreduce(value, rounds):
    kept = []
    for axis, step in rounds:
        upper = (lax.axis_index(axis) // step) % 2 == 1
        half = value.shape[0] // 2
        low, high = value[:half], value[half:]
        keep = jnp.where(upper, high, low)
        value = keep + exchange(jnp.where(upper, low, high), axis, step)
        kept.append((axis, step, upper))
    for axis, step, upper in reversed(kept):
        other = exchange(value, axis, step)
        value = jnp.where(
            upper, jnp.concatenate([other, value]), jnp.concatenate([value, other])
        )
    return value


def a2a_allreduce(value, axes):
    count = 1
    for axis in axes:
        count *= lax.axis_size(axis)
    pieces = value.reshape(count, -1)
    gathered = lax.all_to_all(pieces, axes, 0, 0, tiled=True)
    owned = jnp.sum(gathered, axis=0, keepdims=True)
    spread = jnp.broadcast_to(owned, pieces.shape)
    return lax.all_to_all(spread, axes, 0, 0, tiled=True).reshape(value.shape)


FACTOR_ROUNDS = (("ctx", 1), ("ctx", 2), ("ch", 1), ("ctx", 8), ("ctx", 4), ("ch", 2), ("ch", 4))


def on_device(inputs, norm_gain, conv_taps, factor_one, factor_two, kernel, grad_out):
    local_outer, inner, chans = inputs.shape
    rows = local_outer * inner
    taps_count = conv_taps.shape[1]
    flat_in = inputs.reshape(rows, chans).astype(jnp.float32)
    squares = tree_psum(jnp.sum(flat_in * flat_in, axis=1), "ch")
    inverse = lax.rsqrt(squares / WIDTH + 1e-05)
    hat = flat_in * inverse[:, None]
    normed = (hat * norm_gain).astype(jnp.bfloat16)
    earlier = shifted(normed[rows - (taps_count - 1) :], "ctx", 1)
    extended = jnp.concatenate([earlier, normed], 0)
    value_pre = jnp.zeros((rows, chans), jnp.float32)
    gate_pre = jnp.zeros((rows, chans), jnp.float32)
    for offset in range(taps_count):
        window = extended[taps_count - 1 - offset : taps_count - 1 - offset + rows]
        value_pre = value_pre + conv_taps[0, offset] * window
        gate_pre = gate_pre + conv_taps[1, offset] * window
    mixed_in = value_pre.astype(jnp.bfloat16).reshape(local_outer, inner, chans)
    gate = jax.nn.sigmoid(gate_pre)
    cotangent = grad_out.reshape(rows, chans).astype(jnp.float32)
    section_one = jnp.einsum(
        "ijc,jk->ikc", mixed_in, factor_one, preferred_element_type=jnp.float32
    ).astype(jnp.bfloat16)
    out_grad = (cotangent * gate).astype(jnp.bfloat16).reshape(local_outer, inner, chans)
    columns = lax.all_to_all(section_one, "ctx", split_axis=1, concat_axis=0, tiled=True)
    kern = kernel.astype(jnp.float32)
    spectrum = (columns.astype(jnp.float32) * kern).astype(jnp.bfloat16)
    section_two = jnp.einsum(
        "ijc,ik->kjc", spectrum, factor_two, preferred_element_type=jnp.float32
    ).astype(jnp.bfloat16)
    back_rows = lax.all_to_all(section_two, "ctx", split_axis=0, concat_axis=1, tiled=True)
    grad_columns = lax.all_to_all(out_grad, "ctx", split_axis=1, concat_axis=0, tiled=True)
    grad_spec = jnp.einsum(
        "kjc,ik->ijc", grad_columns, factor_two, preferred_element_type=jnp.float32
    )
    kernel_grad = (grad_spec * columns.astype(jnp.float32)).astype(jnp.bfloat16)
    grad_section = (grad_spec * kern).astype(jnp.bfloat16)
    two_part = jnp.einsum("ijc,kjc->ik", spectrum, grad_columns, preferred_element_type=jnp.float32)
    two_total = tree_allreduce(two_part, FACTOR_ROUNDS)
    back_rows, grad_section = lax.optimization_barrier((back_rows, grad_section))
    grad_rows = lax.all_to_all(grad_section, "ctx", split_axis=0, concat_axis=1, tiled=True)
    back_flat = back_rows.reshape(rows, chans).astype(jnp.float32)
    grad_gate_pre = cotangent * back_flat * gate * (1.0 - gate)
    grad_mixed = jnp.einsum(
        "ikc,jk->ijc", grad_rows, factor_one, preferred_element_type=jnp.float32
    ).reshape(rows, chans)
    one_part = jnp.einsum("ijc,ikc->jk", mixed_in, grad_rows, preferred_element_type=jnp.float32)
    one_total = a2a_allreduce(one_part, ("ctx", "ch"))
    later_value, later_gate = shifted(
        (grad_mixed[: taps_count - 1], grad_gate_pre[: taps_count - 1]), "ctx", -1
    )
    ext_value = jnp.concatenate([grad_mixed, later_value], 0)
    ext_gate = jnp.concatenate([grad_gate_pre, later_gate], 0)
    grad_normed = jnp.zeros((rows, chans), jnp.float32)
    value_taps = []
    gate_taps = []
    for offset in range(taps_count):
        grad_normed = grad_normed + conv_taps[0, offset] * ext_value[offset : offset + rows]
        grad_normed = grad_normed + conv_taps[1, offset] * ext_gate[offset : offset + rows]
        window = extended[taps_count - 1 - offset : taps_count - 1 - offset + rows]
        value_taps.append(jnp.sum(grad_mixed * window, axis=0))
        gate_taps.append(jnp.sum(grad_gate_pre * window, axis=0))
    tap_part = jnp.stack([jnp.stack(value_taps), jnp.stack(gate_taps)])
    gain_part = jnp.sum(grad_normed * hat, axis=0)
    gain_total, taps_total = tree_psum((gain_part, tap_part), "ctx")
    scaled = grad_normed * norm_gain
    row_mean = (
        tree_psum(jnp.sum(scaled * hat, axis=1), "ch")
        / WIDTH
    )
    input_grad = (
        (inverse[:, None] * (scaled - hat * row_mean[:, None]))
        .astype(jnp.bfloat16)
        .reshape(local_outer, inner, chans)
    )
    seq_scale = 1.0 / math.sqrt(OUTER * INNER)
    factor_one_grad = one_total / math.sqrt(OUTER * WIDTH)
    factor_two_grad = two_total / math.sqrt(INNER * WIDTH)
    return (
        input_grad,
        kernel_grad,
        factor_one_grad,
        factor_two_grad,
        gain_total * seq_scale,
        taps_total * seq_scale,
    )


def solution(mesh):
    in_specs = (
        P("ctx", None, "ch"),
        P("ch"),
        P(None, None, "ch"),
        P(),
        P(),
        P(None, "ctx", "ch"),
        P("ctx", None, "ch"),
    )
    out_specs = (P("ctx", None, "ch"), P(None, "ctx", "ch"), P(), P(), P("ch"), P(None, None, "ch"))
    return jax.shard_map(
        on_device, mesh=mesh, in_specs=in_specs, out_specs=out_specs, check_vma=False
    )
```

```python
import math

import jax
import jax.numpy as jnp
from jax import lax
from jax.sharding import PartitionSpec as P

OUTER = 512
INNER = 512
WIDTH = 1024


def shifted(value, axis, steps):
    count = lax.axis_size(axis)
    initial, last = (max(0, -steps), min(count, count - steps))
    return lax.ppermute(value, axis, [(source, source + steps) for source in range(initial, last)])


def tree_psum(value, axis):
    count = lax.axis_size(axis)
    step = 1
    while step < count:
        pairs = [(source, source ^ step) for source in range(count)]
        value = jax.tree.map(lambda v, r: v + r, value, lax.ppermute(value, axis, pairs))
        step *= 2
    return value


def exchange(value, axis, step):
    count = lax.axis_size(axis)
    return lax.ppermute(value, axis, [(source, source ^ step) for source in range(count)])


def tree_allreduce(value, rounds):
    kept = []
    for axis, step in rounds:
        upper = (lax.axis_index(axis) // step) % 2 == 1
        half = value.shape[0] // 2
        low, high = value[:half], value[half:]
        keep = jnp.where(upper, high, low)
        value = keep + exchange(jnp.where(upper, low, high), axis, step)
        kept.append((axis, step, upper))
    for axis, step, upper in reversed(kept):
        other = exchange(value, axis, step)
        value = jnp.where(
            upper, jnp.concatenate([other, value]), jnp.concatenate([value, other])
        )
    return value


FACTOR_ROUNDS = (("ctx", 1), ("ctx", 2), ("ch", 1), ("ctx", 8), ("ctx", 4), ("ch", 2), ("ch", 4))


def on_device(inputs, norm_gain, conv_taps, factor_one, factor_two, kernel, grad_out):
    local_outer, inner, chans = inputs.shape
    rows = local_outer * inner
    taps_count = conv_taps.shape[1]
    flat_in = inputs.reshape(rows, chans).astype(jnp.float32)
    squares = tree_psum(jnp.sum(flat_in * flat_in, axis=1), "ch")
    inverse = lax.rsqrt(squares / WIDTH + 1e-05)
    hat = flat_in * inverse[:, None]
    normed = (hat * norm_gain).astype(jnp.bfloat16)
    earlier = shifted(normed[rows - (taps_count - 1) :], "ctx", 1)
    extended = jnp.concatenate([earlier, normed], 0)
    value_pre = jnp.zeros((rows, chans), jnp.float32)
    gate_pre = jnp.zeros((rows, chans), jnp.float32)
    for offset in range(taps_count):
        window = extended[taps_count - 1 - offset : taps_count - 1 - offset + rows]
        value_pre = value_pre + conv_taps[0, offset] * window
        gate_pre = gate_pre + conv_taps[1, offset] * window
    mixed_in = value_pre.astype(jnp.bfloat16).reshape(local_outer, inner, chans)
    gate = jax.nn.sigmoid(gate_pre)
    cotangent = grad_out.reshape(rows, chans).astype(jnp.float32)
    section_one = jnp.einsum(
        "ijc,jk->ikc", mixed_in, factor_one, preferred_element_type=jnp.float32
    ).astype(jnp.bfloat16)
    out_grad = (cotangent * gate).astype(jnp.bfloat16).reshape(local_outer, inner, chans)
    columns = lax.all_to_all(section_one, "ctx", split_axis=1, concat_axis=0, tiled=True)
    kern = kernel.astype(jnp.float32)
    spectrum = (columns.astype(jnp.float32) * kern).astype(jnp.bfloat16)
    section_two = jnp.einsum(
        "ijc,ik->kjc", spectrum, factor_two, preferred_element_type=jnp.float32
    ).astype(jnp.bfloat16)
    back_rows = lax.all_to_all(section_two, "ctx", split_axis=0, concat_axis=1, tiled=True)
    grad_columns = lax.all_to_all(out_grad, "ctx", split_axis=1, concat_axis=0, tiled=True)
    grad_spec = jnp.einsum(
        "kjc,ik->ijc", grad_columns, factor_two, preferred_element_type=jnp.float32
    )
    kernel_grad = (grad_spec * columns.astype(jnp.float32)).astype(jnp.bfloat16)
    grad_section = (grad_spec * kern).astype(jnp.bfloat16)
    two_part = jnp.einsum("ijc,kjc->ik", spectrum, grad_columns, preferred_element_type=jnp.float32)
    back_rows, grad_section, two_part = lax.optimization_barrier((back_rows, grad_section, two_part))
    grad_rows = lax.all_to_all(grad_section, "ctx", split_axis=0, concat_axis=1, tiled=True)
    back_flat = back_rows.reshape(rows, chans).astype(jnp.float32)
    grad_gate_pre = cotangent * back_flat * gate * (1.0 - gate)
    later_gate = shifted(grad_gate_pre[: taps_count - 1], "ctx", -1)
    ext_gate = jnp.concatenate([grad_gate_pre, later_gate], 0)
    gate_normed = jnp.zeros((rows, chans), jnp.float32)
    gate_taps = []
    for offset in range(taps_count):
        gate_normed = gate_normed + conv_taps[1, offset] * ext_gate[offset : offset + rows]
        window = extended[taps_count - 1 - offset : taps_count - 1 - offset + rows]
        gate_taps.append(jnp.sum(grad_gate_pre * window, axis=0))
    gate_normed, gate_taps, grad_rows = lax.optimization_barrier((gate_normed, gate_taps, grad_rows))
    grad_mixed = jnp.einsum(
        "ikc,jk->ijc", grad_rows, factor_one, preferred_element_type=jnp.float32
    ).reshape(rows, chans)
    one_part = jnp.einsum("ijc,ikc->jk", mixed_in, grad_rows, preferred_element_type=jnp.float32)
    both_total = tree_allreduce(jnp.concatenate([one_part, two_part]), FACTOR_ROUNDS)
    one_total, two_total = both_total[: one_part.shape[0]], both_total[one_part.shape[0] :]
    grad_mixed = lax.optimization_barrier(grad_mixed)
    later_value = shifted(grad_mixed[: taps_count - 1], "ctx", -1)
    ext_value = jnp.concatenate([grad_mixed, later_value], 0)
    grad_normed = gate_normed
    value_taps = []
    for offset in range(taps_count):
        grad_normed = grad_normed + conv_taps[0, offset] * ext_value[offset : offset + rows]
        window = extended[taps_count - 1 - offset : taps_count - 1 - offset + rows]
        value_taps.append(jnp.sum(grad_mixed * window, axis=0))
    tap_part = jnp.stack([jnp.stack(value_taps), jnp.stack(gate_taps)])
    gain_part = jnp.sum(grad_normed * hat, axis=0)
    gain_total, taps_total = tree_psum((gain_part, tap_part), "ctx")
    scaled = grad_normed * norm_gain
    row_mean = (
        tree_psum(jnp.sum(scaled * hat, axis=1), "ch")
        / WIDTH
    )
    input_grad = (
        (inverse[:, None] * (scaled - hat * row_mean[:, None]))
        .astype(jnp.bfloat16)
        .reshape(local_outer, inner, chans)
    )
    seq_scale = 1.0 / math.sqrt(OUTER * INNER)
    factor_one_grad = one_total / math.sqrt(OUTER * WIDTH)
    factor_two_grad = two_total / math.sqrt(INNER * WIDTH)
    return (
        input_grad,
        kernel_grad,
        factor_one_grad,
        factor_two_grad,
        gain_total * seq_scale,
        taps_total * seq_scale,
    )


def solution(mesh):
    in_specs = (
        P("ctx", None, "ch"),
        P("ch"),
        P(None, None, "ch"),
        P(),
        P(),
        P(None, "ctx", "ch"),
        P("ctx", None, "ch"),
    )
    out_specs = (P("ctx", None, "ch"), P(None, "ctx", "ch"), P(), P(), P("ch"), P(None, None, "ch"))
    return jax.shard_map(
        on_device, mesh=mesh, in_specs=in_specs, out_specs=out_specs, check_vma=False
    )
```

```python
import math

import jax
import jax.numpy as jnp
from jax import lax
from jax.sharding import PartitionSpec as P

OUTER = 512
INNER = 512
WIDTH = 1024


def shifted(value, axis, steps):
    count = lax.axis_size(axis)
    initial, last = (max(0, -steps), min(count, count - steps))
    return lax.ppermute(value, axis, [(source, source + steps) for source in range(initial, last)])


def tree_psum(value, axis):
    count = lax.axis_size(axis)
    step = 1
    while step < count:
        pairs = [(source, source ^ step) for source in range(count)]
        value = jax.tree.map(lambda v, r: v + r, value, lax.ppermute(value, axis, pairs))
        step *= 2
    return value


def exchange(value, axis, step):
    count = lax.axis_size(axis)
    return lax.ppermute(value, axis, [(source, source ^ step) for source in range(count)])


def tree_allreduce(value, rounds):
    kept = []
    for axis, step in rounds:
        half = value.shape[0] // 2
        offset = ((lax.axis_index(axis) // step) % 2) * half
        keep = lax.dynamic_slice_in_dim(value, offset, half, 0)
        send = lax.dynamic_slice_in_dim(value, half - offset, half, 0)
        value = keep + exchange(send, axis, step)
        kept.append((axis, step, offset))
    for axis, step, offset in reversed(kept):
        other = exchange(value, axis, step)
        value = lax.dynamic_update_slice_in_dim(jnp.concatenate([other, other]), value, offset, 0)
    return value


FACTOR_ROUNDS = (("ctx", 1), ("ctx", 2), ("ch", 1), ("ctx", 8), ("ctx", 4), ("ch", 2), ("ch", 4))


def on_device(inputs, norm_gain, conv_taps, factor_one, factor_two, kernel, grad_out):
    local_outer, inner, chans = inputs.shape
    rows = local_outer * inner
    taps_count = conv_taps.shape[1]
    flat_in = inputs.reshape(rows, chans).astype(jnp.float32)
    squares = tree_psum(jnp.sum(flat_in * flat_in, axis=1), "ch")
    inverse = lax.rsqrt(squares / WIDTH + 1e-05)
    hat = flat_in * inverse[:, None]
    normed = (hat * norm_gain).astype(jnp.bfloat16)
    earlier = shifted(normed[rows - (taps_count - 1) :], "ctx", 1)
    extended = jnp.concatenate([earlier, normed], 0)
    value_pre = jnp.zeros((rows, chans), jnp.float32)
    gate_pre = jnp.zeros((rows, chans), jnp.float32)
    for offset in range(taps_count):
        window = extended[taps_count - 1 - offset : taps_count - 1 - offset + rows]
        value_pre = value_pre + conv_taps[0, offset] * window
        gate_pre = gate_pre + conv_taps[1, offset] * window
    mixed_in = value_pre.astype(jnp.bfloat16).reshape(local_outer, inner, chans)
    gate = jax.nn.sigmoid(gate_pre)
    cotangent = grad_out.reshape(rows, chans).astype(jnp.float32)
    section_one = jnp.einsum(
        "ijc,jk->ikc", mixed_in, factor_one, preferred_element_type=jnp.float32
    ).astype(jnp.bfloat16)
    out_grad = (cotangent * gate).astype(jnp.bfloat16).reshape(local_outer, inner, chans)
    columns = lax.all_to_all(section_one, "ctx", split_axis=1, concat_axis=0, tiled=True)
    kern = kernel.astype(jnp.float32)
    spectrum = (columns.astype(jnp.float32) * kern).astype(jnp.bfloat16)
    section_two = jnp.einsum(
        "ijc,ik->kjc", spectrum, factor_two, preferred_element_type=jnp.float32
    ).astype(jnp.bfloat16)
    back_rows = lax.all_to_all(section_two, "ctx", split_axis=0, concat_axis=1, tiled=True)
    grad_columns = lax.all_to_all(out_grad, "ctx", split_axis=1, concat_axis=0, tiled=True)
    grad_spec = jnp.einsum(
        "kjc,ik->ijc", grad_columns, factor_two, preferred_element_type=jnp.float32
    )
    kernel_grad = (grad_spec * columns.astype(jnp.float32)).astype(jnp.bfloat16)
    grad_section = (grad_spec * kern).astype(jnp.bfloat16)
    two_part = jnp.einsum("ijc,kjc->ik", spectrum, grad_columns, preferred_element_type=jnp.float32)
    back_rows, grad_section, two_part = lax.optimization_barrier((back_rows, grad_section, two_part))
    grad_rows = lax.all_to_all(grad_section, "ctx", split_axis=0, concat_axis=1, tiled=True)
    back_flat = back_rows.reshape(rows, chans).astype(jnp.float32)
    grad_gate_pre = cotangent * back_flat * gate * (1.0 - gate)
    later_gate = shifted(grad_gate_pre[: taps_count - 1], "ctx", -1)
    ext_gate = jnp.concatenate([grad_gate_pre, later_gate], 0)
    gate_normed = jnp.zeros((rows, chans), jnp.float32)
    gate_taps = []
    for offset in range(taps_count):
        gate_normed = gate_normed + conv_taps[1, offset] * ext_gate[offset : offset + rows]
        window = extended[taps_count - 1 - offset : taps_count - 1 - offset + rows]
        gate_taps.append(jnp.sum(grad_gate_pre * window, axis=0))
    gate_normed, gate_taps, grad_rows = lax.optimization_barrier((gate_normed, gate_taps, grad_rows))
    grad_mixed = jnp.einsum(
        "ikc,jk->ijc", grad_rows, factor_one, preferred_element_type=jnp.float32
    ).reshape(rows, chans)
    one_part = jnp.einsum("ijc,ikc->jk", mixed_in, grad_rows, preferred_element_type=jnp.float32)
    both_total = tree_allreduce(jnp.concatenate([one_part, two_part]), FACTOR_ROUNDS)
    one_total, two_total = both_total[: one_part.shape[0]], both_total[one_part.shape[0] :]
    grad_mixed = lax.optimization_barrier(grad_mixed)
    later_value = shifted(grad_mixed[: taps_count - 1], "ctx", -1)
    ext_value = jnp.concatenate([grad_mixed, later_value], 0)
    grad_normed = gate_normed
    value_taps = []
    for offset in range(taps_count):
        grad_normed = grad_normed + conv_taps[0, offset] * ext_value[offset : offset + rows]
        window = extended[taps_count - 1 - offset : taps_count - 1 - offset + rows]
        value_taps.append(jnp.sum(grad_mixed * window, axis=0))
    tap_part = jnp.stack([jnp.stack(value_taps), jnp.stack(gate_taps)])
    gain_part = jnp.sum(grad_normed * hat, axis=0)
    gain_total, taps_total = tree_psum((gain_part, tap_part), "ctx")
    scaled = grad_normed * norm_gain
    row_mean = (
        tree_psum(jnp.sum(scaled * hat, axis=1), "ch")
        / WIDTH
    )
    input_grad = (
        (inverse[:, None] * (scaled - hat * row_mean[:, None]))
        .astype(jnp.bfloat16)
        .reshape(local_outer, inner, chans)
    )
    seq_scale = 1.0 / math.sqrt(OUTER * INNER)
    factor_one_grad = one_total / math.sqrt(OUTER * WIDTH)
    factor_two_grad = two_total / math.sqrt(INNER * WIDTH)
    return (
        input_grad,
        kernel_grad,
        factor_one_grad,
        factor_two_grad,
        gain_total * seq_scale,
        taps_total * seq_scale,
    )


def solution(mesh):
    in_specs = (
        P("ctx", None, "ch"),
        P("ch"),
        P(None, None, "ch"),
        P(),
        P(),
        P(None, "ctx", "ch"),
        P("ctx", None, "ch"),
    )
    out_specs = (P("ctx", None, "ch"), P(None, "ctx", "ch"), P(), P(), P("ch"), P(None, None, "ch"))
    return jax.shard_map(
        on_device, mesh=mesh, in_specs=in_specs, out_specs=out_specs, check_vma=False
    )
```

```python
import math

import jax
import jax.numpy as jnp
from jax import lax
from jax.sharding import PartitionSpec as P

OUTER = 512
INNER = 512
WIDTH = 1024


def shifted(value, axis, steps):
    count = lax.axis_size(axis)
    initial, last = (max(0, -steps), min(count, count - steps))
    return lax.ppermute(value, axis, [(source, source + steps) for source in range(initial, last)])


def tree_psum(value, axis):
    count = lax.axis_size(axis)
    step = 1
    while step < count:
        pairs = [(source, source ^ step) for source in range(count)]
        value = jax.tree.map(lambda v, r: v + r, value, lax.ppermute(value, axis, pairs))
        step *= 2
    return value


def exchange(value, axis, step):
    count = lax.axis_size(axis)
    return lax.ppermute(value, axis, [(source, source ^ step) for source in range(count)])


def coordinate_bit(spec):
    axis, step = spec
    return (lax.axis_index(axis) // step) % 2


def split_exchange(value, specs, sizes):
    ctx_size, ch_size = sizes
    pairs = []
    for source in range(ctx_size * ch_size):
        row, col = divmod(source, ch_size)
        axis, step = specs[row % 2]
        if axis == "ctx":
            row = row ^ step
        else:
            col = col ^ step
        pairs.append((source, row * ch_size + col))
    return lax.ppermute(value, ("ctx", "ch"), pairs)


def tree_allreduce(value, plan):
    sizes = (lax.axis_size("ctx"), lax.axis_size("ch"))
    on_second = lax.axis_index("ctx") % 2 == 1
    kept = []
    for specs in plan:
        half = value.shape[0] // 2
        bit = jnp.where(on_second, coordinate_bit(specs[1]), coordinate_bit(specs[0]))
        offset = bit * half
        keep = lax.dynamic_slice_in_dim(value, offset, half, 0)
        send = lax.dynamic_slice_in_dim(value, half - offset, half, 0)
        value = keep + split_exchange(send, specs, sizes)
        kept.append((specs, offset))
    for specs, offset in reversed(kept):
        other = split_exchange(value, specs, sizes)
        value = lax.dynamic_update_slice_in_dim(jnp.concatenate([other, other]), value, offset, 0)
    return value


FACTOR_ROUNDS = (
    (("ctx", 1), ("ctx", 1)),
    (("ctx", 2), ("ch", 1)),
    (("ch", 1), ("ctx", 2)),
    (("ctx", 8), ("ctx", 4)),
    (("ctx", 4), ("ctx", 8)),
    (("ch", 2), ("ch", 4)),
    (("ch", 4), ("ch", 2)),
)


def on_device(inputs, norm_gain, conv_taps, factor_one, factor_two, kernel, grad_out):
    local_outer, inner, chans = inputs.shape
    rows = local_outer * inner
    taps_count = conv_taps.shape[1]
    flat_in = inputs.reshape(rows, chans).astype(jnp.float32)
    squares = tree_psum(jnp.sum(flat_in * flat_in, axis=1), "ch")
    inverse = lax.rsqrt(squares / WIDTH + 1e-05)
    hat = flat_in * inverse[:, None]
    normed = (hat * norm_gain).astype(jnp.bfloat16)
    earlier = shifted(normed[rows - (taps_count - 1) :], "ctx", 1)
    extended = jnp.concatenate([earlier, normed], 0)
    value_pre = jnp.zeros((rows, chans), jnp.float32)
    gate_pre = jnp.zeros((rows, chans), jnp.float32)
    for offset in range(taps_count):
        window = extended[taps_count - 1 - offset : taps_count - 1 - offset + rows]
        value_pre = value_pre + conv_taps[0, offset] * window
        gate_pre = gate_pre + conv_taps[1, offset] * window
    mixed_in = value_pre.astype(jnp.bfloat16).reshape(local_outer, inner, chans)
    gate = jax.nn.sigmoid(gate_pre)
    cotangent = grad_out.reshape(rows, chans).astype(jnp.float32)
    section_one = jnp.einsum(
        "ijc,jk->ikc", mixed_in, factor_one, preferred_element_type=jnp.float32
    ).astype(jnp.bfloat16)
    out_grad = (cotangent * gate).astype(jnp.bfloat16).reshape(local_outer, inner, chans)
    columns = lax.all_to_all(section_one, "ctx", split_axis=1, concat_axis=0, tiled=True)
    kern = kernel.astype(jnp.float32)
    spectrum = (columns.astype(jnp.float32) * kern).astype(jnp.bfloat16)
    section_two = jnp.einsum(
        "ijc,ik->kjc", spectrum, factor_two, preferred_element_type=jnp.float32
    ).astype(jnp.bfloat16)
    back_rows = lax.all_to_all(section_two, "ctx", split_axis=0, concat_axis=1, tiled=True)
    grad_columns = lax.all_to_all(out_grad, "ctx", split_axis=1, concat_axis=0, tiled=True)
    grad_spec = jnp.einsum(
        "kjc,ik->ijc", grad_columns, factor_two, preferred_element_type=jnp.float32
    )
    kernel_grad = (grad_spec * columns.astype(jnp.float32)).astype(jnp.bfloat16)
    grad_section = (grad_spec * kern).astype(jnp.bfloat16)
    two_part = jnp.einsum("ijc,kjc->ik", spectrum, grad_columns, preferred_element_type=jnp.float32)
    back_rows, grad_section, two_part = lax.optimization_barrier((back_rows, grad_section, two_part))
    grad_rows = lax.all_to_all(grad_section, "ctx", split_axis=0, concat_axis=1, tiled=True)
    back_flat = back_rows.reshape(rows, chans).astype(jnp.float32)
    grad_gate_pre = cotangent * back_flat * gate * (1.0 - gate)
    later_gate = shifted(grad_gate_pre[: taps_count - 1], "ctx", -1)
    ext_gate = jnp.concatenate([grad_gate_pre, later_gate], 0)
    gate_normed = jnp.zeros((rows, chans), jnp.float32)
    gate_taps = []
    for offset in range(taps_count):
        gate_normed = gate_normed + conv_taps[1, offset] * ext_gate[offset : offset + rows]
        window = extended[taps_count - 1 - offset : taps_count - 1 - offset + rows]
        gate_taps.append(jnp.sum(grad_gate_pre * window, axis=0))
    gate_normed, gate_taps, grad_rows = lax.optimization_barrier((gate_normed, gate_taps, grad_rows))
    grad_mixed = jnp.einsum(
        "ikc,jk->ijc", grad_rows, factor_one, preferred_element_type=jnp.float32
    ).reshape(rows, chans)
    one_part = jnp.einsum("ijc,ikc->jk", mixed_in, grad_rows, preferred_element_type=jnp.float32)
    both_total = tree_allreduce(jnp.concatenate([one_part, two_part]), FACTOR_ROUNDS)
    one_total, two_total = both_total[: one_part.shape[0]], both_total[one_part.shape[0] :]
    grad_mixed = lax.optimization_barrier(grad_mixed)
    later_value = shifted(grad_mixed[: taps_count - 1], "ctx", -1)
    ext_value = jnp.concatenate([grad_mixed, later_value], 0)
    grad_normed = gate_normed
    value_taps = []
    for offset in range(taps_count):
        grad_normed = grad_normed + conv_taps[0, offset] * ext_value[offset : offset + rows]
        window = extended[taps_count - 1 - offset : taps_count - 1 - offset + rows]
        value_taps.append(jnp.sum(grad_mixed * window, axis=0))
    tap_part = jnp.stack([jnp.stack(value_taps), jnp.stack(gate_taps)])
    gain_part = jnp.sum(grad_normed * hat, axis=0)
    gain_total, taps_total = tree_psum((gain_part, tap_part), "ctx")
    scaled = grad_normed * norm_gain
    row_mean = (
        tree_psum(jnp.sum(scaled * hat, axis=1), "ch")
        / WIDTH
    )
    input_grad = (
        (inverse[:, None] * (scaled - hat * row_mean[:, None]))
        .astype(jnp.bfloat16)
        .reshape(local_outer, inner, chans)
    )
    seq_scale = 1.0 / math.sqrt(OUTER * INNER)
    factor_one_grad = one_total / math.sqrt(OUTER * WIDTH)
    factor_two_grad = two_total / math.sqrt(INNER * WIDTH)
    return (
        input_grad,
        kernel_grad,
        factor_one_grad,
        factor_two_grad,
        gain_total * seq_scale,
        taps_total * seq_scale,
    )


def solution(mesh):
    in_specs = (
        P("ctx", None, "ch"),
        P("ch"),
        P(None, None, "ch"),
        P(),
        P(),
        P(None, "ctx", "ch"),
        P("ctx", None, "ch"),
    )
    out_specs = (P("ctx", None, "ch"), P(None, "ctx", "ch"), P(), P(), P("ch"), P(None, None, "ch"))
    return jax.shard_map(
        on_device, mesh=mesh, in_specs=in_specs, out_specs=out_specs, check_vma=False
    )
```

```python
import math

import jax
import jax.numpy as jnp
from jax import lax
from jax.sharding import PartitionSpec as P

OUTER = 512
INNER = 512
WIDTH = 1024


def shifted(value, axis, steps):
    count = lax.axis_size(axis)
    initial, last = (max(0, -steps), min(count, count - steps))
    return lax.ppermute(value, axis, [(source, source + steps) for source in range(initial, last)])


def tree_psum(value, axis):
    count = lax.axis_size(axis)
    step = 1
    while step < count:
        pairs = [(source, source ^ step) for source in range(count)]
        value = jax.tree.map(lambda v, r: v + r, value, lax.ppermute(value, axis, pairs))
        step *= 2
    return value


def exchange(value, axis, step):
    count = lax.axis_size(axis)
    return lax.ppermute(value, axis, [(source, source ^ step) for source in range(count)])


def coordinate_bit(spec):
    axis, step = spec
    return (lax.axis_index(axis) // step) % 2


def split_exchange(value, specs, sizes):
    ctx_size, ch_size = sizes
    pairs = []
    for source in range(ctx_size * ch_size):
        row, col = divmod(source, ch_size)
        axis, step = specs[row % 2]
        if axis == "ctx":
            row = row ^ step
        else:
            col = col ^ step
        pairs.append((source, row * ch_size + col))
    return lax.ppermute(value, ("ctx", "ch"), pairs)


def tree_allreduce(value, plan, fillers=None, state=None):
    fillers = fillers or {}
    sizes = (lax.axis_size("ctx"), lax.axis_size("ch"))
    on_second = lax.axis_index("ctx") % 2 == 1
    kept = []
    for specs in plan:
        half = value.shape[0] // 2
        bit = jnp.where(on_second, coordinate_bit(specs[1]), coordinate_bit(specs[0]))
        offset = bit * half
        keep = lax.dynamic_slice_in_dim(value, offset, half, 0)
        send = lax.dynamic_slice_in_dim(value, half - offset, half, 0)
        received = split_exchange(send, specs, sizes)
        if len(kept) in fillers:
            state = fillers[len(kept)](state)
            received, state = lax.optimization_barrier((received, state))
        value = keep + received
        kept.append((specs, offset))
    for specs, offset in reversed(kept):
        other = split_exchange(value, specs, sizes)
        value = lax.dynamic_update_slice_in_dim(jnp.concatenate([other, other]), value, offset, 0)
    return value, state


FACTOR_ROUNDS = (
    (("ctx", 1), ("ctx", 1)),
    (("ctx", 2), ("ch", 1)),
    (("ch", 1), ("ctx", 2)),
    (("ctx", 8), ("ctx", 4)),
    (("ctx", 4), ("ctx", 8)),
    (("ch", 2), ("ch", 4)),
    (("ch", 4), ("ch", 2)),
)


def on_device(inputs, norm_gain, conv_taps, factor_one, factor_two, kernel, grad_out):
    local_outer, inner, chans = inputs.shape
    rows = local_outer * inner
    taps_count = conv_taps.shape[1]
    flat_in = inputs.reshape(rows, chans).astype(jnp.float32)
    squares = tree_psum(jnp.sum(flat_in * flat_in, axis=1), "ch")
    inverse = lax.rsqrt(squares / WIDTH + 1e-05)
    hat = flat_in * inverse[:, None]
    normed = (hat * norm_gain).astype(jnp.bfloat16)
    earlier = shifted(normed[rows - (taps_count - 1) :], "ctx", 1)
    extended = jnp.concatenate([earlier, normed], 0)
    value_pre = jnp.zeros((rows, chans), jnp.float32)
    gate_pre = jnp.zeros((rows, chans), jnp.float32)
    for offset in range(taps_count):
        window = extended[taps_count - 1 - offset : taps_count - 1 - offset + rows]
        value_pre = value_pre + conv_taps[0, offset] * window
        gate_pre = gate_pre + conv_taps[1, offset] * window
    mixed_in = value_pre.astype(jnp.bfloat16).reshape(local_outer, inner, chans)
    gate = jax.nn.sigmoid(gate_pre)
    cotangent = grad_out.reshape(rows, chans).astype(jnp.float32)
    section_one = jnp.einsum(
        "ijc,jk->ikc", mixed_in, factor_one, preferred_element_type=jnp.float32
    ).astype(jnp.bfloat16)
    out_grad = (cotangent * gate).astype(jnp.bfloat16).reshape(local_outer, inner, chans)
    columns = lax.all_to_all(section_one, "ctx", split_axis=1, concat_axis=0, tiled=True)
    kern = kernel.astype(jnp.float32)
    spectrum = (columns.astype(jnp.float32) * kern).astype(jnp.bfloat16)
    section_two = jnp.einsum(
        "ijc,ik->kjc", spectrum, factor_two, preferred_element_type=jnp.float32
    ).astype(jnp.bfloat16)
    back_rows = lax.all_to_all(section_two, "ctx", split_axis=0, concat_axis=1, tiled=True)
    grad_columns = lax.all_to_all(out_grad, "ctx", split_axis=1, concat_axis=0, tiled=True)
    grad_spec = jnp.einsum(
        "kjc,ik->ijc", grad_columns, factor_two, preferred_element_type=jnp.float32
    )
    kernel_grad = (grad_spec * columns.astype(jnp.float32)).astype(jnp.bfloat16)
    grad_section = (grad_spec * kern).astype(jnp.bfloat16)
    two_part = jnp.einsum("ijc,kjc->ik", spectrum, grad_columns, preferred_element_type=jnp.float32)
    back_rows, grad_section, two_part = lax.optimization_barrier((back_rows, grad_section, two_part))
    grad_rows = lax.all_to_all(grad_section, "ctx", split_axis=0, concat_axis=1, tiled=True)
    back_flat = back_rows.reshape(rows, chans).astype(jnp.float32)
    grad_gate_pre = cotangent * back_flat * gate * (1.0 - gate)
    later_gate = shifted(grad_gate_pre[: taps_count - 1], "ctx", -1)
    ext_gate = jnp.concatenate([grad_gate_pre, later_gate], 0)
    gate_normed = jnp.zeros((rows, chans), jnp.float32)
    gate_taps = []
    for offset in range(taps_count):
        gate_normed = gate_normed + conv_taps[1, offset] * ext_gate[offset : offset + rows]
        window = extended[taps_count - 1 - offset : taps_count - 1 - offset + rows]
        gate_taps.append(jnp.sum(grad_gate_pre * window, axis=0))
    gate_normed, gate_taps, grad_rows = lax.optimization_barrier((gate_normed, gate_taps, grad_rows))
    one_part = jnp.einsum("ijc,ikc->jk", mixed_in, grad_rows, preferred_element_type=jnp.float32)

    def fill_mixed(_):
        return jnp.einsum(
            "ikc,jk->ijc", grad_rows, factor_one, preferred_element_type=jnp.float32
        ).reshape(rows, chans)

    def fill_normed(grad_mixed):
        later_value = shifted(grad_mixed[: taps_count - 1], "ctx", -1)
        ext_value = jnp.concatenate([grad_mixed, later_value], 0)
        grad_normed = gate_normed
        value_taps = []
        for offset in range(taps_count):
            grad_normed = grad_normed + conv_taps[0, offset] * ext_value[offset : offset + rows]
            window = extended[taps_count - 1 - offset : taps_count - 1 - offset + rows]
            value_taps.append(jnp.sum(grad_mixed * window, axis=0))
        scaled = grad_normed * norm_gain
        gain_part = jnp.sum(grad_normed * hat, axis=0)
        return scaled, jnp.sum(scaled * hat, axis=1), value_taps, gain_part

    def fill_rows(state):
        scaled, row_part, value_taps, gain_part = state
        return scaled, tree_psum(row_part, "ch"), value_taps, gain_part

    both_total, (scaled, row_total, value_taps, gain_part) = tree_allreduce(
        jnp.concatenate([one_part, two_part]),
        FACTOR_ROUNDS,
        {1: fill_mixed, 2: fill_normed, 4: fill_rows},
    )
    one_total, two_total = both_total[: one_part.shape[0]], both_total[one_part.shape[0] :]
    tap_part = jnp.stack([jnp.stack(value_taps), jnp.stack(gate_taps)])
    gain_total, taps_total = tree_psum((gain_part, tap_part), "ctx")
    row_mean = row_total / WIDTH
    input_grad = (
        (inverse[:, None] * (scaled - hat * row_mean[:, None]))
        .astype(jnp.bfloat16)
        .reshape(local_outer, inner, chans)
    )
    seq_scale = 1.0 / math.sqrt(OUTER * INNER)
    factor_one_grad = one_total / math.sqrt(OUTER * WIDTH)
    factor_two_grad = two_total / math.sqrt(INNER * WIDTH)
    return (
        input_grad,
        kernel_grad,
        factor_one_grad,
        factor_two_grad,
        gain_total * seq_scale,
        taps_total * seq_scale,
    )


def solution(mesh):
    in_specs = (
        P("ctx", None, "ch"),
        P("ch"),
        P(None, None, "ch"),
        P(),
        P(),
        P(None, "ctx", "ch"),
        P("ctx", None, "ch"),
    )
    out_specs = (P("ctx", None, "ch"), P(None, "ctx", "ch"), P(), P(), P("ch"), P(None, None, "ch"))
    return jax.shard_map(
        on_device, mesh=mesh, in_specs=in_specs, out_specs=out_specs, check_vma=False
    )
```

```python
import math

import jax
import jax.numpy as jnp
from jax import lax
from jax.sharding import PartitionSpec as P

OUTER = 512
INNER = 512
WIDTH = 1024


def shifted(value, axis, steps):
    count = lax.axis_size(axis)
    initial, last = (max(0, -steps), min(count, count - steps))
    return lax.ppermute(value, axis, [(source, source + steps) for source in range(initial, last)])


def tree_psum(value, axis):
    count = lax.axis_size(axis)
    step = 1
    while step < count:
        pairs = [(source, source ^ step) for source in range(count)]
        value = jax.tree.map(lambda v, r: v + r, value, lax.ppermute(value, axis, pairs))
        step *= 2
    return value


def exchange(value, axis, step):
    count = lax.axis_size(axis)
    return lax.ppermute(value, axis, [(source, source ^ step) for source in range(count)])


def coordinate_bit(spec):
    axis, step = spec
    return (lax.axis_index(axis) // step) % 2


def split_exchange(value, specs, sizes):
    ctx_size, ch_size = sizes
    pairs = []
    for source in range(ctx_size * ch_size):
        row, col = divmod(source, ch_size)
        axis, step = specs[row % 2]
        if axis == "ctx":
            row = row ^ step
        else:
            col = col ^ step
        pairs.append((source, row * ch_size + col))
    return lax.ppermute(value, ("ctx", "ch"), pairs)


def tree_allreduce(value, plan, fillers=None, state=None):
    fillers = fillers or {}
    sizes = (lax.axis_size("ctx"), lax.axis_size("ch"))
    on_second = lax.axis_index("ctx") % 2 == 1
    kept = []
    for specs in plan:
        half = value.shape[0] // 2
        bit = jnp.where(on_second, coordinate_bit(specs[1]), coordinate_bit(specs[0]))
        offset = bit * half
        keep = lax.dynamic_slice_in_dim(value, offset, half, 0)
        send = lax.dynamic_slice_in_dim(value, half - offset, half, 0)
        received = split_exchange(send, specs, sizes)
        if len(kept) in fillers:
            state = fillers[len(kept)](state)
            received, state = lax.optimization_barrier((received, state))
        value = keep + received
        kept.append((specs, offset))
    for specs, offset in reversed(kept):
        other = split_exchange(value, specs, sizes)
        value = lax.dynamic_update_slice_in_dim(jnp.concatenate([other, other]), value, offset, 0)
    return value, state


FACTOR_ROUNDS = (
    (("ctx", 1), ("ctx", 1)),
    (("ctx", 2), ("ch", 1)),
    (("ch", 1), ("ctx", 2)),
    (("ctx", 8), ("ctx", 4)),
    (("ctx", 4), ("ctx", 8)),
    (("ch", 2), ("ch", 4)),
    (("ch", 4), ("ch", 2)),
)


def on_device(inputs, norm_gain, conv_taps, factor_one, factor_two, kernel, grad_out):
    local_outer, inner, chans = inputs.shape
    rows = local_outer * inner
    taps_count = conv_taps.shape[1]
    flat_in = inputs.reshape(rows, chans).astype(jnp.float32)
    squares = tree_psum(jnp.sum(flat_in * flat_in, axis=1), "ch")
    inverse = lax.rsqrt(squares / WIDTH + 1e-05)
    hat = flat_in * inverse[:, None]
    normed = (hat * norm_gain).astype(jnp.bfloat16)
    earlier = shifted(normed[rows - (taps_count - 1) :], "ctx", 1)
    extended = jnp.concatenate([earlier, normed], 0)
    value_pre = jnp.zeros((rows, chans), jnp.float32)
    gate_pre = jnp.zeros((rows, chans), jnp.float32)
    for offset in range(taps_count):
        window = extended[taps_count - 1 - offset : taps_count - 1 - offset + rows]
        value_pre = value_pre + conv_taps[0, offset] * window
        gate_pre = gate_pre + conv_taps[1, offset] * window
    mixed_in = value_pre.astype(jnp.bfloat16).reshape(local_outer, inner, chans)
    gate = jax.nn.sigmoid(gate_pre)
    cotangent = grad_out.reshape(rows, chans).astype(jnp.float32)
    section_one = jnp.einsum(
        "ijc,jk->ikc", mixed_in, factor_one, preferred_element_type=jnp.float32
    ).astype(jnp.bfloat16)
    out_grad = (cotangent * gate).astype(jnp.bfloat16).reshape(local_outer, inner, chans)
    columns = lax.all_to_all(section_one, "ctx", split_axis=1, concat_axis=0, tiled=True)
    kern = kernel.astype(jnp.float32)
    spectrum = (columns.astype(jnp.float32) * kern).astype(jnp.bfloat16)
    section_two = jnp.einsum(
        "ijc,ik->kjc", spectrum, factor_two, preferred_element_type=jnp.float32
    ).astype(jnp.bfloat16)
    grad_columns = lax.all_to_all(out_grad, "ctx", split_axis=1, concat_axis=0, tiled=True)
    grad_spec = jnp.einsum(
        "kjc,ik->ijc", grad_columns, factor_two, preferred_element_type=jnp.float32
    )
    kernel_grad = (grad_spec * columns.astype(jnp.float32)).astype(jnp.bfloat16)
    grad_section = (grad_spec * kern).astype(jnp.bfloat16)
    two_part = jnp.einsum("ijc,kjc->ik", spectrum, grad_columns, preferred_element_type=jnp.float32)
    grad_rows = lax.all_to_all(grad_section, "ctx", split_axis=0, concat_axis=1, tiled=True)
    grad_rows, section_two, two_part = lax.optimization_barrier((grad_rows, section_two, two_part))
    back_rows = lax.all_to_all(section_two, "ctx", split_axis=0, concat_axis=1, tiled=True)
    one_part = jnp.einsum("ijc,ikc->jk", mixed_in, grad_rows, preferred_element_type=jnp.float32)
    grad_mixed = jnp.einsum(
        "ikc,jk->ijc", grad_rows, factor_one, preferred_element_type=jnp.float32
    ).reshape(rows, chans)
    later_value = shifted(grad_mixed[: taps_count - 1], "ctx", -1)
    ext_value = jnp.concatenate([grad_mixed, later_value], 0)
    value_normed = jnp.zeros((rows, chans), jnp.float32)
    value_taps = []
    for offset in range(taps_count):
        value_normed = value_normed + conv_taps[0, offset] * ext_value[offset : offset + rows]
        window = extended[taps_count - 1 - offset : taps_count - 1 - offset + rows]
        value_taps.append(jnp.sum(grad_mixed * window, axis=0))
    value_normed, value_taps, one_part, back_rows = lax.optimization_barrier(
        (value_normed, value_taps, one_part, back_rows)
    )

    def fill_normed(_):
        back_flat = back_rows.reshape(rows, chans).astype(jnp.float32)
        grad_gate_pre = cotangent * back_flat * gate * (1.0 - gate)
        later_gate = shifted(grad_gate_pre[: taps_count - 1], "ctx", -1)
        ext_gate = jnp.concatenate([grad_gate_pre, later_gate], 0)
        grad_normed = value_normed
        gate_taps = []
        for offset in range(taps_count):
            grad_normed = grad_normed + conv_taps[1, offset] * ext_gate[offset : offset + rows]
            window = extended[taps_count - 1 - offset : taps_count - 1 - offset + rows]
            gate_taps.append(jnp.sum(grad_gate_pre * window, axis=0))
        scaled = grad_normed * norm_gain
        gain_part = jnp.sum(grad_normed * hat, axis=0)
        return scaled, jnp.sum(scaled * hat, axis=1), gate_taps, gain_part

    def fill_rows(state):
        scaled, row_part, gate_taps, gain_part = state
        return scaled, tree_psum(row_part, "ch"), gate_taps, gain_part

    both_total, (scaled, row_total, gate_taps, gain_part) = tree_allreduce(
        jnp.concatenate([one_part, two_part]),
        FACTOR_ROUNDS,
        {1: fill_normed, 3: fill_rows},
    )
    one_total, two_total = both_total[: one_part.shape[0]], both_total[one_part.shape[0] :]
    tap_part = jnp.stack([jnp.stack(value_taps), jnp.stack(gate_taps)])
    gain_total, taps_total = tree_psum((gain_part, tap_part), "ctx")
    row_mean = row_total / WIDTH
    input_grad = (
        (inverse[:, None] * (scaled - hat * row_mean[:, None]))
        .astype(jnp.bfloat16)
        .reshape(local_outer, inner, chans)
    )
    seq_scale = 1.0 / math.sqrt(OUTER * INNER)
    factor_one_grad = one_total / math.sqrt(OUTER * WIDTH)
    factor_two_grad = two_total / math.sqrt(INNER * WIDTH)
    return (
        input_grad,
        kernel_grad,
        factor_one_grad,
        factor_two_grad,
        gain_total * seq_scale,
        taps_total * seq_scale,
    )


def solution(mesh):
    in_specs = (
        P("ctx", None, "ch"),
        P("ch"),
        P(None, None, "ch"),
        P(),
        P(),
        P(None, "ctx", "ch"),
        P("ctx", None, "ch"),
    )
    out_specs = (P("ctx", None, "ch"), P(None, "ctx", "ch"), P(), P(), P("ch"), P(None, None, "ch"))
    return jax.shard_map(
        on_device, mesh=mesh, in_specs=in_specs, out_specs=out_specs, check_vma=False
    )
```

```python
import math

import jax
import jax.numpy as jnp
from jax import lax
from jax.sharding import PartitionSpec as P

OUTER = 512
INNER = 512
WIDTH = 1024


def shifted(value, axis, steps):
    count = lax.axis_size(axis)
    initial, last = (max(0, -steps), min(count, count - steps))
    return lax.ppermute(value, axis, [(source, source + steps) for source in range(initial, last)])


def tree_psum(value, axis):
    count = lax.axis_size(axis)
    step = 1
    while step < count:
        pairs = [(source, source ^ step) for source in range(count)]
        value = jax.tree.map(lambda v, r: v + r, value, lax.ppermute(value, axis, pairs))
        step *= 2
    return value


def exchange(value, axis, step):
    count = lax.axis_size(axis)
    return lax.ppermute(value, axis, [(source, source ^ step) for source in range(count)])


def coordinate_bit(spec):
    axis, step = spec
    return (lax.axis_index(axis) // step) % 2


def group_digit(group):
    digit = 0
    for place, (axis, step) in enumerate(group):
        digit = digit + ((lax.axis_index(axis) // step) % 2) * (1 << place)
    return digit


def group_exchange(value, groups, shift, sizes):
    ctx_size, ch_size = sizes
    pairs = []
    for source in range(ctx_size * ch_size):
        row, col = divmod(source, ch_size)
        for place, (axis, step) in enumerate(groups[row % 2]):
            if shift >> place & 1:
                if axis == "ctx":
                    row = row ^ step
                else:
                    col = col ^ step
        pairs.append((source, row * ch_size + col))
    return lax.ppermute(value, ("ctx", "ch"), pairs)


def tree_allreduce(value, plan, fillers=None, state=None):
    fillers = fillers or {}
    sizes = (lax.axis_size("ctx"), lax.axis_size("ch"))
    on_second = lax.axis_index("ctx") % 2 == 1
    kept = []
    for groups in plan:
        count = 1 << len(groups[0])
        digit = jnp.where(on_second, group_digit(groups[1]), group_digit(groups[0]))
        pieces = value.reshape((count, value.shape[0] // count) + value.shape[1:])
        total = pieces[digit]
        received = [
            group_exchange(pieces[digit ^ shift], groups, shift, sizes) for shift in range(1, count)
        ]
        if len(kept) in fillers:
            state = fillers[len(kept)](state)
            received, state = lax.optimization_barrier((received, state))
        for part in received:
            total = total + part
        value = total
        kept.append((groups, count, digit))
    for groups, count, digit in reversed(kept):
        parts = [value] + [group_exchange(value, groups, shift, sizes) for shift in range(1, count)]
        order = jnp.arange(count) ^ digit
        value = jnp.take(jnp.stack(parts), order, axis=0).reshape((-1,) + value.shape[1:])
    return value, state


Y_GROUP = (("ctx", 2), ("ctx", 4))
X_GROUP = (("ch", 1), ("ch", 2))
Z_GROUP = (("ctx", 8), ("ch", 4))
FACTOR_ROUNDS = (
    ((("ctx", 1),), (("ctx", 1),)),
    (Y_GROUP, X_GROUP),
    (X_GROUP, Y_GROUP),
    (Z_GROUP, Z_GROUP),
)


def on_device(inputs, norm_gain, conv_taps, factor_one, factor_two, kernel, grad_out):
    local_outer, inner, chans = inputs.shape
    rows = local_outer * inner
    taps_count = conv_taps.shape[1]
    flat_in = inputs.reshape(rows, chans).astype(jnp.float32)
    squares = tree_psum(jnp.sum(flat_in * flat_in, axis=1), "ch")
    inverse = lax.rsqrt(squares / WIDTH + 1e-05)
    hat = flat_in * inverse[:, None]
    normed = (hat * norm_gain).astype(jnp.bfloat16)
    earlier = shifted(normed[rows - (taps_count - 1) :], "ctx", 1)
    extended = jnp.concatenate([earlier, normed], 0)
    value_pre = jnp.zeros((rows, chans), jnp.float32)
    gate_pre = jnp.zeros((rows, chans), jnp.float32)
    for offset in range(taps_count):
        window = extended[taps_count - 1 - offset : taps_count - 1 - offset + rows]
        value_pre = value_pre + conv_taps[0, offset] * window
        gate_pre = gate_pre + conv_taps[1, offset] * window
    mixed_in = value_pre.astype(jnp.bfloat16).reshape(local_outer, inner, chans)
    gate = jax.nn.sigmoid(gate_pre)
    cotangent = grad_out.reshape(rows, chans).astype(jnp.float32)
    section_one = jnp.einsum(
        "ijc,jk->ikc", mixed_in, factor_one, preferred_element_type=jnp.float32
    ).astype(jnp.bfloat16)
    out_grad = (cotangent * gate).astype(jnp.bfloat16).reshape(local_outer, inner, chans)
    columns = lax.all_to_all(section_one, "ctx", split_axis=1, concat_axis=0, tiled=True)
    kern = kernel.astype(jnp.float32)
    spectrum = (columns.astype(jnp.float32) * kern).astype(jnp.bfloat16)
    section_two = jnp.einsum(
        "ijc,ik->kjc", spectrum, factor_two, preferred_element_type=jnp.float32
    ).astype(jnp.bfloat16)
    back_rows = lax.all_to_all(section_two, "ctx", split_axis=0, concat_axis=1, tiled=True)
    grad_columns = lax.all_to_all(out_grad, "ctx", split_axis=1, concat_axis=0, tiled=True)
    grad_spec = jnp.einsum(
        "kjc,ik->ijc", grad_columns, factor_two, preferred_element_type=jnp.float32
    )
    kernel_grad = (grad_spec * columns.astype(jnp.float32)).astype(jnp.bfloat16)
    grad_section = (grad_spec * kern).astype(jnp.bfloat16)
    two_part = jnp.einsum("ijc,kjc->ik", spectrum, grad_columns, preferred_element_type=jnp.float32)
    back_rows, grad_section, two_part = lax.optimization_barrier((back_rows, grad_section, two_part))
    grad_rows = lax.all_to_all(grad_section, "ctx", split_axis=0, concat_axis=1, tiled=True)
    back_flat = back_rows.reshape(rows, chans).astype(jnp.float32)
    grad_gate_pre = cotangent * back_flat * gate * (1.0 - gate)
    later_gate = shifted(grad_gate_pre[: taps_count - 1], "ctx", -1)
    ext_gate = jnp.concatenate([grad_gate_pre, later_gate], 0)
    gate_normed = jnp.zeros((rows, chans), jnp.float32)
    gate_taps = []
    for offset in range(taps_count):
        gate_normed = gate_normed + conv_taps[1, offset] * ext_gate[offset : offset + rows]
        window = extended[taps_count - 1 - offset : taps_count - 1 - offset + rows]
        gate_taps.append(jnp.sum(grad_gate_pre * window, axis=0))
    gate_normed, gate_taps, grad_rows = lax.optimization_barrier((gate_normed, gate_taps, grad_rows))
    one_part = jnp.einsum("ijc,ikc->jk", mixed_in, grad_rows, preferred_element_type=jnp.float32)

    def fill_mixed(_):
        return jnp.einsum(
            "ikc,jk->ijc", grad_rows, factor_one, preferred_element_type=jnp.float32
        ).reshape(rows, chans)

    def fill_normed(grad_mixed):
        later_value = shifted(grad_mixed[: taps_count - 1], "ctx", -1)
        ext_value = jnp.concatenate([grad_mixed, later_value], 0)
        grad_normed = gate_normed
        value_taps = []
        for offset in range(taps_count):
            grad_normed = grad_normed + conv_taps[0, offset] * ext_value[offset : offset + rows]
            window = extended[taps_count - 1 - offset : taps_count - 1 - offset + rows]
            value_taps.append(jnp.sum(grad_mixed * window, axis=0))
        scaled = grad_normed * norm_gain
        gain_part = jnp.sum(grad_normed * hat, axis=0)
        return scaled, jnp.sum(scaled * hat, axis=1), value_taps, gain_part

    def fill_rows(state):
        scaled, row_part, value_taps, gain_part = state
        return scaled, tree_psum(row_part, "ch"), value_taps, gain_part

    both_total, (scaled, row_total, value_taps, gain_part) = tree_allreduce(
        jnp.concatenate([one_part, two_part]),
        FACTOR_ROUNDS,
        {1: fill_mixed, 2: fill_normed, 3: fill_rows},
    )
    one_total, two_total = both_total[: one_part.shape[0]], both_total[one_part.shape[0] :]
    tap_part = jnp.stack([jnp.stack(value_taps), jnp.stack(gate_taps)])
    gain_total, taps_total = tree_psum((gain_part, tap_part), "ctx")
    row_mean = row_total / WIDTH
    input_grad = (
        (inverse[:, None] * (scaled - hat * row_mean[:, None]))
        .astype(jnp.bfloat16)
        .reshape(local_outer, inner, chans)
    )
    seq_scale = 1.0 / math.sqrt(OUTER * INNER)
    factor_one_grad = one_total / math.sqrt(OUTER * WIDTH)
    factor_two_grad = two_total / math.sqrt(INNER * WIDTH)
    return (
        input_grad,
        kernel_grad,
        factor_one_grad,
        factor_two_grad,
        gain_total * seq_scale,
        taps_total * seq_scale,
    )


def solution(mesh):
    in_specs = (
        P("ctx", None, "ch"),
        P("ch"),
        P(None, None, "ch"),
        P(),
        P(),
        P(None, "ctx", "ch"),
        P("ctx", None, "ch"),
    )
    out_specs = (P("ctx", None, "ch"), P(None, "ctx", "ch"), P(), P(), P("ch"), P(None, None, "ch"))
    return jax.shard_map(
        on_device, mesh=mesh, in_specs=in_specs, out_specs=out_specs, check_vma=False
    )
```

```python
import math

import jax
import jax.numpy as jnp
from jax import lax
from jax.sharding import PartitionSpec as P

OUTER = 512
INNER = 512
WIDTH = 1024


def shifted(value, axis, steps):
    count = lax.axis_size(axis)
    initial, last = (max(0, -steps), min(count, count - steps))
    return lax.ppermute(value, axis, [(source, source + steps) for source in range(initial, last)])


def tree_psum(value, axis):
    count = lax.axis_size(axis)
    order = jnp.arange(count) ^ lax.axis_index(axis)

    def total(leaf):
        parts = [leaf] + [
            lax.ppermute(leaf, axis, [(source, source ^ shift) for source in range(count)])
            for shift in range(1, count)
        ]
        return jnp.sum(jnp.take(jnp.stack(parts), order, axis=0), axis=0)

    return jax.tree.map(total, value)


def exchange(value, axis, step):
    count = lax.axis_size(axis)
    return lax.ppermute(value, axis, [(source, source ^ step) for source in range(count)])


def coordinate_bit(spec):
    axis, step = spec
    return (lax.axis_index(axis) // step) % 2


def group_digit(group):
    digit = 0
    for place, (axis, step) in enumerate(group):
        digit = digit + ((lax.axis_index(axis) // step) % 2) * (1 << place)
    return digit


def group_exchange(value, groups, shift, sizes):
    ctx_size, ch_size = sizes
    pairs = []
    for source in range(ctx_size * ch_size):
        row, col = divmod(source, ch_size)
        for place, (axis, step) in enumerate(groups[row % 2]):
            if shift >> place & 1:
                if axis == "ctx":
                    row = row ^ step
                else:
                    col = col ^ step
        pairs.append((source, row * ch_size + col))
    return lax.ppermute(value, ("ctx", "ch"), pairs)


def tree_allreduce(value, plan, fillers=None, state=None):
    fillers = fillers or {}
    sizes = (lax.axis_size("ctx"), lax.axis_size("ch"))
    on_second = lax.axis_index("ctx") % 2 == 1
    kept = []
    for groups in plan:
        count = 1 << len(groups[0])
        digit = jnp.where(on_second, group_digit(groups[1]), group_digit(groups[0]))
        pieces = value.reshape((count, value.shape[0] // count) + value.shape[1:])
        total = pieces[digit]
        received = [
            group_exchange(pieces[digit ^ shift], groups, shift, sizes) for shift in range(1, count)
        ]
        if len(kept) in fillers:
            state = fillers[len(kept)](state)
            received, state = lax.optimization_barrier((received, state))
        for part in received:
            total = total + part
        value = total
        kept.append((groups, count, digit))
    for groups, count, digit in reversed(kept):
        parts = [value] + [group_exchange(value, groups, shift, sizes) for shift in range(1, count)]
        order = jnp.arange(count) ^ digit
        value = jnp.take(jnp.stack(parts), order, axis=0).reshape((-1,) + value.shape[1:])
    return value, state


Y_GROUP = (("ctx", 2), ("ctx", 4))
X_GROUP = (("ch", 1), ("ch", 2))
Z_GROUP = (("ctx", 8), ("ch", 4))
FACTOR_ROUNDS = (
    ((("ctx", 1),), (("ctx", 1),)),
    (Y_GROUP, X_GROUP),
    (X_GROUP, Y_GROUP),
    (Z_GROUP, Z_GROUP),
)


def on_device(inputs, norm_gain, conv_taps, factor_one, factor_two, kernel, grad_out):
    local_outer, inner, chans = inputs.shape
    rows = local_outer * inner
    taps_count = conv_taps.shape[1]
    flat_in = inputs.reshape(rows, chans).astype(jnp.float32)
    squares = tree_psum(jnp.sum(flat_in * flat_in, axis=1), "ch")
    inverse = lax.rsqrt(squares / WIDTH + 1e-05)
    hat = flat_in * inverse[:, None]
    normed = (hat * norm_gain).astype(jnp.bfloat16)
    earlier = shifted(normed[rows - (taps_count - 1) :], "ctx", 1)
    extended = jnp.concatenate([earlier, normed], 0)
    value_pre = jnp.zeros((rows, chans), jnp.float32)
    gate_pre = jnp.zeros((rows, chans), jnp.float32)
    for offset in range(taps_count):
        window = extended[taps_count - 1 - offset : taps_count - 1 - offset + rows]
        value_pre = value_pre + conv_taps[0, offset] * window
        gate_pre = gate_pre + conv_taps[1, offset] * window
    mixed_in = value_pre.astype(jnp.bfloat16).reshape(local_outer, inner, chans)
    gate = jax.nn.sigmoid(gate_pre)
    cotangent = grad_out.reshape(rows, chans).astype(jnp.float32)
    section_one = jnp.einsum(
        "ijc,jk->ikc", mixed_in, factor_one, preferred_element_type=jnp.float32
    ).astype(jnp.bfloat16)
    out_grad = (cotangent * gate).astype(jnp.bfloat16).reshape(local_outer, inner, chans)
    columns = lax.all_to_all(section_one, "ctx", split_axis=1, concat_axis=0, tiled=True)
    kern = kernel.astype(jnp.float32)
    spectrum = (columns.astype(jnp.float32) * kern).astype(jnp.bfloat16)
    section_two = jnp.einsum(
        "ijc,ik->kjc", spectrum, factor_two, preferred_element_type=jnp.float32
    ).astype(jnp.bfloat16)
    back_rows = lax.all_to_all(section_two, "ctx", split_axis=0, concat_axis=1, tiled=True)
    grad_columns = lax.all_to_all(out_grad, "ctx", split_axis=1, concat_axis=0, tiled=True)
    grad_spec = jnp.einsum(
        "kjc,ik->ijc", grad_columns, factor_two, preferred_element_type=jnp.float32
    )
    kernel_grad = (grad_spec * columns.astype(jnp.float32)).astype(jnp.bfloat16)
    grad_section = (grad_spec * kern).astype(jnp.bfloat16)
    two_part = jnp.einsum("ijc,kjc->ik", spectrum, grad_columns, preferred_element_type=jnp.float32)
    back_rows, grad_section, two_part = lax.optimization_barrier((back_rows, grad_section, two_part))
    grad_rows = lax.all_to_all(grad_section, "ctx", split_axis=0, concat_axis=1, tiled=True)
    back_flat = back_rows.reshape(rows, chans).astype(jnp.float32)
    grad_gate_pre = cotangent * back_flat * gate * (1.0 - gate)
    later_gate = shifted(grad_gate_pre[: taps_count - 1], "ctx", -1)
    ext_gate = jnp.concatenate([grad_gate_pre, later_gate], 0)
    gate_normed = jnp.zeros((rows, chans), jnp.float32)
    gate_taps = []
    for offset in range(taps_count):
        gate_normed = gate_normed + conv_taps[1, offset] * ext_gate[offset : offset + rows]
        window = extended[taps_count - 1 - offset : taps_count - 1 - offset + rows]
        gate_taps.append(jnp.sum(grad_gate_pre * window, axis=0))
    gate_normed, gate_taps, grad_rows = lax.optimization_barrier((gate_normed, gate_taps, grad_rows))
    one_part = jnp.einsum("ijc,ikc->jk", mixed_in, grad_rows, preferred_element_type=jnp.float32)

    def fill_mixed(_):
        return jnp.einsum(
            "ikc,jk->ijc", grad_rows, factor_one, preferred_element_type=jnp.float32
        ).reshape(rows, chans)

    def fill_normed(grad_mixed):
        later_value = shifted(grad_mixed[: taps_count - 1], "ctx", -1)
        ext_value = jnp.concatenate([grad_mixed, later_value], 0)
        grad_normed = gate_normed
        value_taps = []
        for offset in range(taps_count):
            grad_normed = grad_normed + conv_taps[0, offset] * ext_value[offset : offset + rows]
            window = extended[taps_count - 1 - offset : taps_count - 1 - offset + rows]
            value_taps.append(jnp.sum(grad_mixed * window, axis=0))
        scaled = grad_normed * norm_gain
        gain_part = jnp.sum(grad_normed * hat, axis=0)
        return scaled, jnp.sum(scaled * hat, axis=1), value_taps, gain_part

    def fill_rows(state):
        scaled, row_part, value_taps, gain_part = state
        return scaled, tree_psum(row_part, "ch"), value_taps, gain_part

    both_total, (scaled, row_total, value_taps, gain_part) = tree_allreduce(
        jnp.concatenate([one_part, two_part]),
        FACTOR_ROUNDS,
        {1: fill_mixed, 2: fill_normed, 3: fill_rows},
    )
    one_total, two_total = both_total[: one_part.shape[0]], both_total[one_part.shape[0] :]
    tap_part = jnp.stack([jnp.stack(value_taps), jnp.stack(gate_taps)])
    gain_total, taps_total = tree_psum((gain_part, tap_part), "ctx")
    row_mean = row_total / WIDTH
    input_grad = (
        (inverse[:, None] * (scaled - hat * row_mean[:, None]))
        .astype(jnp.bfloat16)
        .reshape(local_outer, inner, chans)
    )
    seq_scale = 1.0 / math.sqrt(OUTER * INNER)
    factor_one_grad = one_total / math.sqrt(OUTER * WIDTH)
    factor_two_grad = two_total / math.sqrt(INNER * WIDTH)
    return (
        input_grad,
        kernel_grad,
        factor_one_grad,
        factor_two_grad,
        gain_total * seq_scale,
        taps_total * seq_scale,
    )


def solution(mesh):
    in_specs = (
        P("ctx", None, "ch"),
        P("ch"),
        P(None, None, "ch"),
        P(),
        P(),
        P(None, "ctx", "ch"),
        P("ctx", None, "ch"),
    )
    out_specs = (P("ctx", None, "ch"), P(None, "ctx", "ch"), P(), P(), P("ch"), P(None, None, "ch"))
    return jax.shard_map(
        on_device, mesh=mesh, in_specs=in_specs, out_specs=out_specs, check_vma=False
    )
```

```python
import math

import jax
import jax.numpy as jnp
from jax import lax
from jax.sharding import PartitionSpec as P

OUTER = 512
INNER = 512
WIDTH = 1024


def shifted(value, axis, steps):
    count = lax.axis_size(axis)
    initial, last = (max(0, -steps), min(count, count - steps))
    return lax.ppermute(value, axis, [(source, source + steps) for source in range(initial, last)])


def tree_psum(value, axis):
    count = lax.axis_size(axis)
    step = 1
    while step < count:
        width = 4 if step * 4 <= count else 2
        digit = (lax.axis_index(axis) // step) % width
        order = jnp.arange(width) ^ digit

        def total(leaf):
            parts = [leaf] + [
                lax.ppermute(
                    leaf, axis, [(source, source ^ (shift * step)) for source in range(count)]
                )
                for shift in range(1, width)
            ]
            return jnp.sum(jnp.take(jnp.stack(parts), order, axis=0), axis=0)

        value = jax.tree.map(total, value)
        step *= width
    return value


def exchange(value, axis, step):
    count = lax.axis_size(axis)
    return lax.ppermute(value, axis, [(source, source ^ step) for source in range(count)])


def coordinate_bit(spec):
    axis, step = spec
    return (lax.axis_index(axis) // step) % 2


def group_digit(group):
    digit = 0
    for place, (axis, step) in enumerate(group):
        digit = digit + ((lax.axis_index(axis) // step) % 2) * (1 << place)
    return digit


def group_exchange(value, groups, shift, sizes):
    ctx_size, ch_size = sizes
    pairs = []
    for source in range(ctx_size * ch_size):
        row, col = divmod(source, ch_size)
        for place, (axis, step) in enumerate(groups[row % 2]):
            if shift >> place & 1:
                if axis == "ctx":
                    row = row ^ step
                else:
                    col = col ^ step
        pairs.append((source, row * ch_size + col))
    return lax.ppermute(value, ("ctx", "ch"), pairs)


def tree_allreduce(value, plan, fillers=None, state=None):
    fillers = fillers or {}
    sizes = (lax.axis_size("ctx"), lax.axis_size("ch"))
    on_second = lax.axis_index("ctx") % 2 == 1
    kept = []
    for groups in plan:
        count = 1 << len(groups[0])
        digit = jnp.where(on_second, group_digit(groups[1]), group_digit(groups[0]))
        pieces = value.reshape((count, value.shape[0] // count) + value.shape[1:])
        total = pieces[digit]
        received = [
            group_exchange(pieces[digit ^ shift], groups, shift, sizes) for shift in range(1, count)
        ]
        if len(kept) in fillers:
            state = fillers[len(kept)](state)
            received, state = lax.optimization_barrier((received, state))
        for part in received:
            total = total + part
        value = total
        kept.append((groups, count, digit))
    for groups, count, digit in reversed(kept):
        parts = [value] + [group_exchange(value, groups, shift, sizes) for shift in range(1, count)]
        order = jnp.arange(count) ^ digit
        value = jnp.take(jnp.stack(parts), order, axis=0).reshape((-1,) + value.shape[1:])
    return value, state


Y_GROUP = (("ctx", 2), ("ctx", 4))
X_GROUP = (("ch", 1), ("ch", 2))
Z_GROUP = (("ctx", 8), ("ch", 4))
FACTOR_ROUNDS = (
    ((("ctx", 1),), (("ctx", 1),)),
    (Y_GROUP, X_GROUP),
    (X_GROUP, Y_GROUP),
    (Z_GROUP, Z_GROUP),
)


def on_device(inputs, norm_gain, conv_taps, factor_one, factor_two, kernel, grad_out):
    local_outer, inner, chans = inputs.shape
    rows = local_outer * inner
    taps_count = conv_taps.shape[1]
    flat_in = inputs.reshape(rows, chans).astype(jnp.float32)
    squares = tree_psum(jnp.sum(flat_in * flat_in, axis=1), "ch")
    inverse = lax.rsqrt(squares / WIDTH + 1e-05)
    hat = flat_in * inverse[:, None]
    normed = (hat * norm_gain).astype(jnp.bfloat16)
    earlier = shifted(normed[rows - (taps_count - 1) :], "ctx", 1)
    extended = jnp.concatenate([earlier, normed], 0)
    value_pre = jnp.zeros((rows, chans), jnp.float32)
    gate_pre = jnp.zeros((rows, chans), jnp.float32)
    for offset in range(taps_count):
        window = extended[taps_count - 1 - offset : taps_count - 1 - offset + rows]
        value_pre = value_pre + conv_taps[0, offset] * window
        gate_pre = gate_pre + conv_taps[1, offset] * window
    mixed_in = value_pre.astype(jnp.bfloat16).reshape(local_outer, inner, chans)
    gate = jax.nn.sigmoid(gate_pre)
    cotangent = grad_out.reshape(rows, chans).astype(jnp.float32)
    section_one = jnp.einsum(
        "ijc,jk->ikc", mixed_in, factor_one, preferred_element_type=jnp.float32
    ).astype(jnp.bfloat16)
    out_grad = (cotangent * gate).astype(jnp.bfloat16).reshape(local_outer, inner, chans)
    columns = lax.all_to_all(section_one, "ctx", split_axis=1, concat_axis=0, tiled=True)
    kern = kernel.astype(jnp.float32)
    spectrum = (columns.astype(jnp.float32) * kern).astype(jnp.bfloat16)
    section_two = jnp.einsum(
        "ijc,ik->kjc", spectrum, factor_two, preferred_element_type=jnp.float32
    ).astype(jnp.bfloat16)
    back_rows = lax.all_to_all(section_two, "ctx", split_axis=0, concat_axis=1, tiled=True)
    grad_columns = lax.all_to_all(out_grad, "ctx", split_axis=1, concat_axis=0, tiled=True)
    grad_spec = jnp.einsum(
        "kjc,ik->ijc", grad_columns, factor_two, preferred_element_type=jnp.float32
    )
    kernel_grad = (grad_spec * columns.astype(jnp.float32)).astype(jnp.bfloat16)
    grad_section = (grad_spec * kern).astype(jnp.bfloat16)
    two_part = jnp.einsum("ijc,kjc->ik", spectrum, grad_columns, preferred_element_type=jnp.float32)
    back_rows, grad_section, two_part = lax.optimization_barrier((back_rows, grad_section, two_part))
    grad_rows = lax.all_to_all(grad_section, "ctx", split_axis=0, concat_axis=1, tiled=True)
    back_flat = back_rows.reshape(rows, chans).astype(jnp.float32)
    grad_gate_pre = cotangent * back_flat * gate * (1.0 - gate)
    later_gate = shifted(grad_gate_pre[: taps_count - 1], "ctx", -1)
    ext_gate = jnp.concatenate([grad_gate_pre, later_gate], 0)
    gate_normed = jnp.zeros((rows, chans), jnp.float32)
    gate_taps = []
    for offset in range(taps_count):
        gate_normed = gate_normed + conv_taps[1, offset] * ext_gate[offset : offset + rows]
        window = extended[taps_count - 1 - offset : taps_count - 1 - offset + rows]
        gate_taps.append(jnp.sum(grad_gate_pre * window, axis=0))
    gate_normed, gate_taps, grad_rows = lax.optimization_barrier((gate_normed, gate_taps, grad_rows))
    one_part = jnp.einsum("ijc,ikc->jk", mixed_in, grad_rows, preferred_element_type=jnp.float32)

    def fill_mixed(_):
        return jnp.einsum(
            "ikc,jk->ijc", grad_rows, factor_one, preferred_element_type=jnp.float32
        ).reshape(rows, chans)

    def fill_normed(grad_mixed):
        later_value = shifted(grad_mixed[: taps_count - 1], "ctx", -1)
        ext_value = jnp.concatenate([grad_mixed, later_value], 0)
        grad_normed = gate_normed
        value_taps = []
        for offset in range(taps_count):
            grad_normed = grad_normed + conv_taps[0, offset] * ext_value[offset : offset + rows]
            window = extended[taps_count - 1 - offset : taps_count - 1 - offset + rows]
            value_taps.append(jnp.sum(grad_mixed * window, axis=0))
        scaled = grad_normed * norm_gain
        gain_part = jnp.sum(grad_normed * hat, axis=0)
        return scaled, jnp.sum(scaled * hat, axis=1), value_taps, gain_part

    def fill_rows(state):
        scaled, row_part, value_taps, gain_part = state
        return scaled, tree_psum(row_part, "ch"), value_taps, gain_part

    both_total, (scaled, row_total, value_taps, gain_part) = tree_allreduce(
        jnp.concatenate([one_part, two_part]),
        FACTOR_ROUNDS,
        {1: fill_mixed, 2: fill_normed, 3: fill_rows},
    )
    one_total, two_total = both_total[: one_part.shape[0]], both_total[one_part.shape[0] :]
    tap_part = jnp.stack([jnp.stack(value_taps), jnp.stack(gate_taps)])
    gain_total, taps_total = tree_psum((gain_part, tap_part), "ctx")
    row_mean = row_total / WIDTH
    input_grad = (
        (inverse[:, None] * (scaled - hat * row_mean[:, None]))
        .astype(jnp.bfloat16)
        .reshape(local_outer, inner, chans)
    )
    seq_scale = 1.0 / math.sqrt(OUTER * INNER)
    factor_one_grad = one_total / math.sqrt(OUTER * WIDTH)
    factor_two_grad = two_total / math.sqrt(INNER * WIDTH)
    return (
        input_grad,
        kernel_grad,
        factor_one_grad,
        factor_two_grad,
        gain_total * seq_scale,
        taps_total * seq_scale,
    )


def solution(mesh):
    in_specs = (
        P("ctx", None, "ch"),
        P("ch"),
        P(None, None, "ch"),
        P(),
        P(),
        P(None, "ctx", "ch"),
        P("ctx", None, "ch"),
    )
    out_specs = (P("ctx", None, "ch"), P(None, "ctx", "ch"), P(), P(), P("ch"), P(None, None, "ch"))
    return jax.shard_map(
        on_device, mesh=mesh, in_specs=in_specs, out_specs=out_specs, check_vma=False
    )
```

```python
import math

import jax
import jax.numpy as jnp
from jax import lax
from jax.sharding import PartitionSpec as P

OUTER = 512
INNER = 512
WIDTH = 1024


def shifted(value, axis, steps):
    count = lax.axis_size(axis)
    initial, last = (max(0, -steps), min(count, count - steps))
    return lax.ppermute(value, axis, [(source, source + steps) for source in range(initial, last)])


def tree_psum(value, axis):
    count = lax.axis_size(axis)
    step = 1
    while step < count:
        pairs = [(source, source ^ step) for source in range(count)]
        value = jax.tree.map(lambda v, r: v + r, value, lax.ppermute(value, axis, pairs))
        step *= 2
    return value


def exchange(value, axis, step):
    count = lax.axis_size(axis)
    return lax.ppermute(value, axis, [(source, source ^ step) for source in range(count)])


def coordinate_bit(spec):
    axis, step = spec
    return (lax.axis_index(axis) // step) % 2


def group_digit(group):
    digit = 0
    for place, (axis, step) in enumerate(group):
        digit = digit + ((lax.axis_index(axis) // step) % 2) * (1 << place)
    return digit


def group_exchange(value, groups, shift, sizes):
    ctx_size, ch_size = sizes
    pairs = []
    for source in range(ctx_size * ch_size):
        row, col = divmod(source, ch_size)
        for place, (axis, step) in enumerate(groups[row % 2]):
            if shift >> place & 1:
                if axis == "ctx":
                    row = row ^ step
                else:
                    col = col ^ step
        pairs.append((source, row * ch_size + col))
    return lax.ppermute(value, ("ctx", "ch"), pairs)


def tree_allreduce(value, plan, fillers=None, state=None):
    fillers = fillers or {}
    sizes = (lax.axis_size("ctx"), lax.axis_size("ch"))
    on_second = lax.axis_index("ctx") % 2 == 1
    kept = []
    for groups in plan:
        count = 1 << len(groups[0])
        digit = jnp.where(on_second, group_digit(groups[1]), group_digit(groups[0]))
        pieces = value.reshape((count, value.shape[0] // count) + value.shape[1:])
        total = pieces[digit]
        received = [
            group_exchange(pieces[digit ^ shift], groups, shift, sizes) for shift in range(1, count)
        ]
        if len(kept) in fillers:
            state = fillers[len(kept)](state)
            received, state = lax.optimization_barrier((received, state))
        for part in received:
            total = total + part
        value = total
        kept.append((groups, count, digit))
    for groups, count, digit in reversed(kept):
        parts = [value] + [group_exchange(value, groups, shift, sizes) for shift in range(1, count)]
        order = jnp.arange(count) ^ digit
        value = jnp.take(jnp.stack(parts), order, axis=0).reshape((-1,) + value.shape[1:])
    return value, state


Y_GROUP = (("ctx", 2), ("ctx", 4))
X_GROUP = (("ch", 1), ("ch", 2))
Z_GROUP = (("ctx", 8), ("ch", 4))
FACTOR_ROUNDS = (
    ((("ctx", 1),), (("ctx", 1),)),
    (Y_GROUP, X_GROUP),
    (X_GROUP, Y_GROUP),
    (Z_GROUP, Z_GROUP),
)


def on_device(inputs, norm_gain, conv_taps, factor_one, factor_two, kernel, grad_out):
    local_outer, inner, chans = inputs.shape
    rows = local_outer * inner
    taps_count = conv_taps.shape[1]
    flat_in = inputs.reshape(rows, chans).astype(jnp.float32)
    squares = tree_psum(jnp.sum(flat_in * flat_in, axis=1), "ch")
    inverse = lax.rsqrt(squares / WIDTH + 1e-05)
    hat = flat_in * inverse[:, None]
    normed = (hat * norm_gain).astype(jnp.bfloat16)
    earlier = shifted(normed[rows - (taps_count - 1) :], "ctx", 1)
    extended = jnp.concatenate([earlier, normed], 0)
    value_pre = jnp.zeros((rows, chans), jnp.float32)
    gate_pre = jnp.zeros((rows, chans), jnp.float32)
    for offset in range(taps_count):
        window = extended[taps_count - 1 - offset : taps_count - 1 - offset + rows]
        value_pre = value_pre + conv_taps[0, offset] * window
        gate_pre = gate_pre + conv_taps[1, offset] * window
    mixed_in = value_pre.astype(jnp.bfloat16).reshape(local_outer, inner, chans)
    gate = jax.nn.sigmoid(gate_pre)
    cotangent = grad_out.reshape(rows, chans).astype(jnp.float32)
    section_one = jnp.einsum(
        "ijc,jk->ikc", mixed_in, factor_one, preferred_element_type=jnp.float32
    ).astype(jnp.bfloat16)
    out_grad = (cotangent * gate).astype(jnp.bfloat16).reshape(local_outer, inner, chans)
    columns = lax.all_to_all(section_one, "ctx", split_axis=1, concat_axis=0, tiled=True)
    kern = kernel.astype(jnp.float32)
    spectrum = (columns.astype(jnp.float32) * kern).astype(jnp.bfloat16)
    section_two = jnp.einsum(
        "ijc,ik->kjc", spectrum, factor_two, preferred_element_type=jnp.float32
    ).astype(jnp.bfloat16)
    back_rows = lax.all_to_all(section_two, "ctx", split_axis=0, concat_axis=1, tiled=True)
    grad_columns = lax.all_to_all(out_grad, "ctx", split_axis=1, concat_axis=0, tiled=True)
    grad_spec = jnp.einsum(
        "kjc,ik->ijc", grad_columns, factor_two, preferred_element_type=jnp.float32
    )
    kernel_grad = (grad_spec * columns.astype(jnp.float32)).astype(jnp.bfloat16)
    grad_section = (grad_spec * kern).astype(jnp.bfloat16)
    two_part = jnp.einsum("ijc,kjc->ik", spectrum, grad_columns, preferred_element_type=jnp.float32)
    back_rows, grad_section, two_part = lax.optimization_barrier((back_rows, grad_section, two_part))
    grad_rows = lax.all_to_all(grad_section, "ctx", split_axis=0, concat_axis=1, tiled=True)
    back_flat = back_rows.reshape(rows, chans).astype(jnp.float32)
    grad_gate_pre = cotangent * back_flat * gate * (1.0 - gate)
    later_gate = shifted(grad_gate_pre[: taps_count - 1], "ctx", -1)
    ext_gate = jnp.concatenate([grad_gate_pre, later_gate], 0)
    gate_normed = jnp.zeros((rows, chans), jnp.float32)
    gate_taps = []
    for offset in range(taps_count):
        gate_normed = gate_normed + conv_taps[1, offset] * ext_gate[offset : offset + rows]
        window = extended[taps_count - 1 - offset : taps_count - 1 - offset + rows]
        gate_taps.append(jnp.sum(grad_gate_pre * window, axis=0))
    gate_normed, gate_taps, grad_rows = lax.optimization_barrier((gate_normed, gate_taps, grad_rows))
    one_part = jnp.einsum("ijc,ikc->jk", mixed_in, grad_rows, preferred_element_type=jnp.float32)

    def fill_mixed(_):
        return jnp.einsum(
            "ikc,jk->ijc", grad_rows, factor_one, preferred_element_type=jnp.float32
        ).reshape(rows, chans)

    def fill_normed(grad_mixed):
        later_value = shifted(grad_mixed[: taps_count - 1], "ctx", -1)
        ext_value = jnp.concatenate([grad_mixed, later_value], 0)
        grad_normed = gate_normed
        value_taps = []
        for offset in range(taps_count):
            grad_normed = grad_normed + conv_taps[0, offset] * ext_value[offset : offset + rows]
            window = extended[taps_count - 1 - offset : taps_count - 1 - offset + rows]
            value_taps.append(jnp.sum(grad_mixed * window, axis=0))
        scaled = grad_normed * norm_gain
        gain_part = jnp.sum(grad_normed * hat, axis=0)
        return scaled, jnp.sum(scaled * hat, axis=1), value_taps, gain_part

    def fill_rows(state):
        scaled, row_part, value_taps, gain_part = state
        return scaled, tree_psum(row_part, "ch"), value_taps, gain_part

    both_total, (scaled, row_total, value_taps, gain_part) = tree_allreduce(
        jnp.concatenate([one_part, two_part]),
        FACTOR_ROUNDS,
        {1: fill_mixed, 2: fill_normed, 3: fill_rows},
    )
    one_total, two_total = both_total[: one_part.shape[0]], both_total[one_part.shape[0] :]
    tap_part = jnp.stack([jnp.stack(value_taps), jnp.stack(gate_taps)])
    packed = tree_psum(jnp.concatenate([gain_part[None], tap_part.reshape(-1, chans)]), "ctx")
    gain_total, taps_total = packed[0], packed[1:].reshape(tap_part.shape)
    row_mean = row_total / WIDTH
    input_grad = (
        (inverse[:, None] * (scaled - hat * row_mean[:, None]))
        .astype(jnp.bfloat16)
        .reshape(local_outer, inner, chans)
    )
    seq_scale = 1.0 / math.sqrt(OUTER * INNER)
    factor_one_grad = one_total / math.sqrt(OUTER * WIDTH)
    factor_two_grad = two_total / math.sqrt(INNER * WIDTH)
    return (
        input_grad,
        kernel_grad,
        factor_one_grad,
        factor_two_grad,
        gain_total * seq_scale,
        taps_total * seq_scale,
    )


def solution(mesh):
    in_specs = (
        P("ctx", None, "ch"),
        P("ch"),
        P(None, None, "ch"),
        P(),
        P(),
        P(None, "ctx", "ch"),
        P("ctx", None, "ch"),
    )
    out_specs = (P("ctx", None, "ch"), P(None, "ctx", "ch"), P(), P(), P("ch"), P(None, None, "ch"))
    return jax.shard_map(
        on_device, mesh=mesh, in_specs=in_specs, out_specs=out_specs, check_vma=False
    )
```
